32 devices in a mesh: grp: 4 (over y, x), blk: 8 (over z, core).
Axes of the slice: x: 2, y: 2, z: 4, core: 2. Of those that a mesh axis runs over, the one named last changes fastest.
Arguments:
- voltages: bfloat16 [4096, 188416], P(('blk', 'grp')), may hold values from -6 to 6
- filter_taps: float32 [8, 8192], replicated, may hold values from -0.0234375 to 0.0234375
- channel_index: int32 [16], replicated, may hold values from 0 to 4095
- antenna_slot_order: int32 [2048], replicated, may hold values from 0 to 2047, each once
Outputs:
- visibilities: bfloat16 [16, 4096, 2, 4096], P('grp', 'blk')
The draws below stay inside these ranges and needn't reach their ends.
All inputs are finite; a program needn't handle non-finite values.
Results may differ from the reference program's by a relative error of at most 0.0065.
Values sent between devices are 32-bit elements; how exact they have to be, the bound alone decides.
No kernel may reach another device: no remote copies, remote signals or barrier semaphores. Data moves between devices by JAX's collectives and lax.ppermute only.
A program may use at most 192 MiB of HBM per device.

```python
import math
import jax
import jax.numpy as jnp
from jax import lax

ANTENNA_COUNT = 2048
NFFT = 8192
TAPS = 8
CH = 16
SPEC = 16
INPUTS = 4096
SAMPLES = 188416


def with_ends(result, key, smallest, high):
    longest = result.shape.index(max(result.shape))
    spots = []
    for shift in (0, 1):
        where = [jax.random.randint(jax.random.fold_in(key, axis), (), 0, length) for axis, length in enumerate(result.shape)]
        where[longest] = (where[longest] + shift) % result.shape[longest]
        spots.append(tuple(where))
    return result.at[spots[0]].set(smallest).at[spots[1]].set(high)


def steps_of(rng, shape, cuts, smallest, largest):
    def one(dim, shards_of):
        steps = jax.random.uniform(jax.random.fold_in(jax.random.fold_in(rng, 6), dim), (shards_of,), jnp.float32, smallest / len(cuts), largest / len(cuts))
        return jnp.repeat(jnp.exp(steps), shape[dim] // shards_of).reshape((-1,) + (1,) * (len(shape) - dim - 1))

    loudness = one(*cuts[0])
    for cut in cuts[1:]:
        loudness = loudness * one(*cut)
    return loudness


def bell_draw(rng, dims, scale, most, shards=(), held_as=jnp.bfloat16):
    result = jax.random.normal(rng, dims, jnp.float32) * scale
    if len(shards) > 0:
        result = steps_of(rng, dims, shards, -0.22, 0.18) * result
    return jnp.clip(result, min=-most, max=most).astype(held_as)


def setup_inputs(seed: int = 0) -> dict:
    key_list = jax.random.split(jax.random.key(seed), 5)
    return {
        "voltages": bell_draw(key_list[0], (INPUTS, SAMPLES), 1.0, 6.0, ((0, 32),)),
        "filter_taps": bell_draw(key_list[1], (TAPS, NFFT), (TAPS * NFFT) ** -0.5, 0.0234375, (), jnp.float32),
        "channel_index": with_ends(jax.random.randint(key_list[2], (CH,), 0, NFFT // 2), jax.random.fold_in(key_list[2], 1), 0, (NFFT // 2) - 1).astype(jnp.int32),
        "antenna_slot_order": jax.random.permutation(key_list[3], ANTENNA_COUNT).astype(jnp.int32),
    }


def phase_table(channel_index, fft_length):
    samples_idx = jnp.arange(fft_length, dtype=jnp.int32)
    phase = (samples_idx[:, None] * channel_index[None, :].astype(jnp.int32)) % fft_length
    angle = phase.astype(jnp.float32) * jnp.float32(2.0 * math.pi / fft_length)
    return jnp.concatenate([jnp.cos(angle), -jnp.sin(angle)], axis=1).astype(jnp.bfloat16)


def channelize(voltages, filter_taps, channel_index):
    tap_count, fft_length = filter_taps.shape
    row_count = voltages.shape[0]
    frame_count = voltages.shape[1] // fft_length
    spectra = frame_count - tap_count + 1
    blocked = voltages.reshape(row_count, frame_count, fft_length)
    filtered = jnp.zeros((row_count, spectra, fft_length), jnp.float32)
    for tap_index in range(tap_count):
        filtered = filtered + filter_taps[tap_index][None, None, :] * blocked[:, tap_index:tap_index + spectra, :].astype(jnp.float32)
    twiddle = phase_table(channel_index, fft_length)
    spectrum = jnp.dot(filtered.astype(jnp.bfloat16).reshape(row_count * spectra, fft_length), twiddle, preferred_element_type=jnp.float32)
    chan_count = channel_index.shape[0]
    return spectrum.reshape(row_count, spectra, 2, chan_count).transpose(3, 2, 1, 0).reshape(chan_count, 2 * spectra, row_count)


def column_index(antenna_slot_order):
    count = antenna_slot_order.shape[0]
    inverse = jnp.zeros((count,), jnp.int32).at[antenna_slot_order].set(jnp.arange(count, dtype=jnp.int32))
    column_entry = jnp.arange(2 * count, dtype=jnp.int32)
    return 2 * inverse[column_entry // 2] + column_entry % 2


def stacked_rows(block):
    half = block.shape[1] // 2
    turned = jnp.concatenate([block[:, half:], -block[:, :half]], axis=1)
    return jnp.stack([block, turned], axis=1)


def reference(voltages, filter_taps, channel_index, antenna_slot_order):
    rows_per_block = 128 if INPUTS % 128 == 0 else INPUTS
    grouped_rows = voltages.reshape(INPUTS // rows_per_block, rows_per_block, SAMPLES)
    pieces = lax.map(lambda part_rows: channelize(part_rows, filter_taps, channel_index), grouped_rows)
    spectra_all = jnp.moveaxis(pieces, 0, 2).reshape(CH, 2 * SPEC, INPUTS)
    columns = column_index(antenna_slot_order)
    ordered = jnp.take(spectra_all, columns, axis=2)
    lhs_all = stacked_rows(spectra_all)
    scale = jnp.float32(1.0 / SPEC)

    def one_channel(pair):
        left_operand_single, cols_one = pair
        product = jnp.einsum("pkr,kn->rpn", left_operand_single, cols_one, precision=lax.Precision.HIGHEST, preferred_element_type=jnp.float32)
        return (product * scale).astype(jnp.bfloat16)

    return lax.map(one_channel, (lhs_all, ordered))
```

```python
import math

import jax
import jax.numpy as jnp
from jax import lax
from jax.experimental import pallas as pl
from jax.experimental.pallas import tpu as pltpu
from jax.sharding import PartitionSpec as P


def phase_table(channel_index, fft_length):
    samples_idx = jnp.arange(fft_length, dtype=jnp.int32)
    phase = samples_idx[:, None] * channel_index[None, :] % fft_length
    angle = phase.astype(jnp.float32) * jnp.float32(2.0 * math.pi / fft_length)
    return jnp.concatenate([jnp.cos(angle), -jnp.sin(angle)], axis=1).astype(jnp.bfloat16)


def _frame_kernel(v_ref, w_ref, o_ref):
    o_ref[0] = jnp.dot(v_ref[...], w_ref[...], preferred_element_type=jnp.float32)


def frame_products(voltages, weights, fft_length):
    rows, samples = voltages.shape
    frames = samples // fft_length
    width = weights.shape[1]
    return pl.pallas_call(
        _frame_kernel,
        grid=(frames,),
        in_specs=[
            pl.BlockSpec((rows, fft_length), lambda f: (0, f)),
            pl.BlockSpec((fft_length, width), lambda f: (0, 0)),
        ],
        out_specs=pl.BlockSpec((1, rows, width), lambda f: (f, 0, 0)),
        out_shape=jax.ShapeDtypeStruct((frames, rows, width), jnp.float32),
        compiler_params=pltpu.CompilerParams(vmem_limit_bytes=48 * 1024 * 1024),
    )(voltages, weights)


def channelize(voltages, filter_taps, channel_index):
    tap_count, fft_length = filter_taps.shape
    frame_count = voltages.shape[1] // fft_length
    spectra = frame_count - tap_count + 1
    twiddle = phase_table(channel_index, fft_length).astype(jnp.float32)
    cols = twiddle.shape[1]
    weights = (filter_taps[:, :, None] * twiddle[None, :, :]).astype(jnp.bfloat16)
    weights = weights.transpose(1, 0, 2).reshape(fft_length, tap_count * cols)
    prod = frame_products(voltages, weights, fft_length)
    spec = prod[0:spectra, :, 0:cols]
    for m in range(1, tap_count):
        spec = spec + prod[m : m + spectra, :, m * cols : (m + 1) * cols]
    return spec


def column_index(antenna_slot_order):
    count = antenna_slot_order.shape[0]
    ids = jnp.arange(count, dtype=jnp.int32)
    inverse = jnp.sum(
        jnp.where(antenna_slot_order[None, :] == ids[:, None], ids[None, :], 0), axis=1
    )
    column_entry = jnp.arange(2 * count, dtype=jnp.int32)
    return 2 * inverse[column_entry // 2] + column_entry % 2


def split2(x):
    hi = x.astype(jnp.bfloat16)
    lo = (x - hi.astype(jnp.float32)).astype(jnp.bfloat16)
    return hi, lo


def _corr_kernel(l0_ref, l1_ref, o_ref, out_ref):
    rhs = o_ref[0]
    r0 = jnp.dot(l0_ref[0], rhs, preferred_element_type=jnp.float32)
    r1 = jnp.dot(l1_ref[0], rhs, preferred_element_type=jnp.float32)
    out_ref[0] = jnp.stack([r0, r1], axis=1).astype(out_ref.dtype)


def correlate(l0, l1, rhs, block_rows):
    chans, slots, width = l0.shape
    cols = rhs.shape[2]
    return pl.pallas_call(
        _corr_kernel,
        grid=(chans, slots // block_rows),
        in_specs=[
            pl.BlockSpec((1, block_rows, width), lambda c, s: (c, s, 0)),
            pl.BlockSpec((1, block_rows, width), lambda c, s: (c, s, 0)),
            pl.BlockSpec((1, width, cols), lambda c, s: (c, 0, 0)),
        ],
        out_specs=pl.BlockSpec((1, block_rows, 2, cols), lambda c, s: (c, s, 0, 0)),
        out_shape=jax.ShapeDtypeStruct((chans, slots, 2, cols), jnp.bfloat16),
        compiler_params=pltpu.CompilerParams(vmem_limit_bytes=48 * 1024 * 1024),
    )(l0, l1, rhs)


def per_device(voltages, filter_taps, channel_index, antenna_slot_order):
    spec = channelize(voltages, filter_taps, channel_index)
    spectra, rows, cols = spec.shape
    chans = cols // 2
    grp = lax.psum(1, "grp")
    local_ch = chans // grp
    x = spec.reshape(spectra, rows, 2, chans).transpose(1, 3, 2, 0)
    x = lax.all_to_all(x, "grp", split_axis=1, concat_axis=0, tiled=True)
    slots_local = x.shape[0]
    x = x.reshape(slots_local, local_ch * 2 * spectra)
    everything = lax.all_gather(x, "blk", axis=0, tiled=True)
    columns = column_index(antenna_slot_order)
    ordered = jnp.take(everything, columns, axis=0)
    ordered = ordered.reshape(-1, local_ch, 2 * spectra).transpose(1, 0, 2)
    scale = jnp.float32(1.0 / spectra)
    xl = x.reshape(slots_local, local_ch, 2, spectra).transpose(1, 0, 2, 3) * scale
    re = xl[:, :, 0, :]
    im = xl[:, :, 1, :]
    row0 = jnp.concatenate([re, im], axis=-1)
    row1 = jnp.concatenate([im, -re], axis=-1)
    r0a, r0b = split2(row0)
    r1a, r1b = split2(row1)
    o1, o2 = split2(ordered)
    l0 = jnp.concatenate([r0a, r0a, r0b], axis=-1)
    l1 = jnp.concatenate([r1a, r1a, r1b], axis=-1)
    rhs = jnp.concatenate([o1, o2, o1], axis=-1).transpose(0, 2, 1)
    result = correlate(l0, l1, rhs, min(128, slots_local))
    return result


def solution(mesh):
    in_specs = (P(("blk", "grp"), None), P(), P(), P())
    out_specs = P("grp", "blk", None, None)
    return jax.shard_map(
        per_device, mesh=mesh, in_specs=in_specs, out_specs=out_specs, check_vma=False
    )
```

```python
import math

import jax
import jax.numpy as jnp
from jax import lax
from jax.experimental import pallas as pl
from jax.experimental.pallas import tpu as pltpu
from jax.sharding import PartitionSpec as P


def phase_table(channel_index, fft_length):
    samples_idx = jnp.arange(fft_length, dtype=jnp.int32)
    phase = samples_idx[:, None] * channel_index[None, :] % fft_length
    angle = phase.astype(jnp.float32) * jnp.float32(2.0 * math.pi / fft_length)
    return jnp.concatenate([jnp.cos(angle), -jnp.sin(angle)], axis=1).astype(jnp.bfloat16)


def _frame_kernel(v_ref, w_ref, o_ref):
    n = w_ref.shape[0]
    group = o_ref.shape[0]
    lhs = jnp.concatenate([v_ref[:, g * n : (g + 1) * n] for g in range(group)], axis=0)
    res = jnp.dot(lhs, w_ref[...], preferred_element_type=jnp.float32)
    o_ref[...] = res.reshape(o_ref.shape)


def frame_products(voltages, weights, fft_length, group):
    rows, samples = voltages.shape
    frames = samples // fft_length
    steps = -(-frames // group)
    width = weights.shape[1]
    return pl.pallas_call(
        _frame_kernel,
        grid=(steps,),
        in_specs=[
            pl.BlockSpec((rows, group * fft_length), lambda f: (0, f)),
            pl.BlockSpec((fft_length, width), lambda f: (0, 0)),
        ],
        out_specs=pl.BlockSpec((group, rows, width), lambda f: (f, 0, 0)),
        out_shape=jax.ShapeDtypeStruct((steps * group, rows, width), jnp.float32),
        compiler_params=pltpu.CompilerParams(vmem_limit_bytes=56 * 1024 * 1024),
    )(voltages, weights)


def channelize(voltages, filter_taps, channel_index):
    tap_count, fft_length = filter_taps.shape
    frame_count = voltages.shape[1] // fft_length
    spectra = frame_count - tap_count + 1
    twiddle = phase_table(channel_index, fft_length).astype(jnp.float32)
    cols = twiddle.shape[1]
    weights = (filter_taps[:, :, None] * twiddle[None, :, :]).astype(jnp.bfloat16)
    weights = weights.transpose(1, 0, 2).reshape(fft_length, tap_count * cols)
    prod = frame_products(voltages, weights, fft_length, 4)
    spec = prod[0:spectra, :, 0:cols]
    for m in range(1, tap_count):
        spec = spec + prod[m : m + spectra, :, m * cols : (m + 1) * cols]
    return spec


def column_index(antenna_slot_order):
    count = antenna_slot_order.shape[0]
    ids = jnp.arange(count, dtype=jnp.int32)
    inverse = jnp.sum(
        jnp.where(antenna_slot_order[None, :] == ids[:, None], ids[None, :], 0), axis=1
    )
    pol = jnp.arange(2, dtype=jnp.int32)
    return (2 * inverse[:, None] + pol[None, :]).reshape(2 * count)


def split2(x):
    hi = x.astype(jnp.bfloat16)
    lo = (x - hi.astype(jnp.float32)).astype(jnp.bfloat16)
    return hi, lo


def _corr_kernel(l_ref, o_ref, out_ref):
    res = jnp.dot(l_ref[0], o_ref[0], preferred_element_type=jnp.float32)
    out_ref[0] = res.astype(out_ref.dtype).reshape(out_ref.shape[1:])


def correlate(lhs, rhs, block_rows):
    chans, slots, pairs, width = lhs.shape
    cols = rhs.shape[2]
    lhs = lhs.reshape(chans, slots * pairs, width)
    return pl.pallas_call(
        _corr_kernel,
        grid=(chans, slots // block_rows),
        in_specs=[
            pl.BlockSpec((1, block_rows * pairs, width), lambda c, s: (c, s, 0)),
            pl.BlockSpec((1, width, cols), lambda c, s: (c, 0, 0)),
        ],
        out_specs=pl.BlockSpec((1, block_rows, pairs, cols), lambda c, s: (c, s, 0, 0)),
        out_shape=jax.ShapeDtypeStruct((chans, slots, pairs, cols), jnp.bfloat16),
        compiler_params=pltpu.CompilerParams(vmem_limit_bytes=48 * 1024 * 1024),
    )(lhs, rhs)


def per_device(voltages, filter_taps, channel_index, antenna_slot_order):
    spec = channelize(voltages, filter_taps, channel_index)
    spectra, rows, cols = spec.shape
    chans = cols // 2
    grp = lax.psum(1, "grp")
    local_ch = chans // grp
    x = spec.reshape(spectra, rows, 2, chans).transpose(1, 3, 2, 0)
    x = lax.all_to_all(x, "grp", split_axis=1, concat_axis=0, tiled=True)
    slots_local = x.shape[0]
    x = x.reshape(slots_local, local_ch * 2 * spectra)
    everything = lax.all_gather(x, "blk", axis=0, tiled=True)
    columns = column_index(antenna_slot_order)
    ordered = jnp.take(everything, columns, axis=0)
    ordered = ordered.reshape(-1, local_ch, 2 * spectra).transpose(1, 0, 2)
    scale = jnp.float32(1.0 / spectra)
    xl = x.reshape(slots_local, local_ch, 2, spectra).transpose(1, 0, 2, 3) * scale
    re = xl[:, :, 0, :]
    im = xl[:, :, 1, :]
    row0 = jnp.concatenate([re, im], axis=-1)
    row1 = jnp.concatenate([im, -re], axis=-1)
    lhs = jnp.stack([row0, row1], axis=2)
    la, lb = split2(lhs)
    o1, o2 = split2(ordered)
    lcat = jnp.concatenate([la, la, lb], axis=-1)
    rhs = jnp.concatenate([o1, o2, o1], axis=-1).transpose(0, 2, 1)
    result = correlate(lcat, rhs, min(128, slots_local))
    return result


def solution(mesh):
    in_specs = (P(("blk", "grp"), None), P(), P(), P())
    out_specs = P("grp", "blk", None, None)
    return jax.shard_map(
        per_device, mesh=mesh, in_specs=in_specs, out_specs=out_specs, check_vma=False
    )
```

```python
import math

import jax
import jax.numpy as jnp
from jax import lax
from jax.experimental import pallas as pl
from jax.experimental.pallas import tpu as pltpu
from jax.sharding import PartitionSpec as P


def phase_table(channel_index, fft_length):
    samples_idx = jnp.arange(fft_length, dtype=jnp.int32)
    phase = samples_idx[:, None] * channel_index[None, :] % fft_length
    angle = phase.astype(jnp.float32) * jnp.float32(2.0 * math.pi / fft_length)
    return jnp.concatenate([jnp.cos(angle), -jnp.sin(angle)], axis=1).astype(jnp.bfloat16)


def phase_table_t(channel_index, fft_length):
    samples_idx = jnp.arange(fft_length, dtype=jnp.int32)
    phase = channel_index[:, None] * samples_idx[None, :] % fft_length
    angle = phase.astype(jnp.float32) * jnp.float32(2.0 * math.pi / fft_length)
    return jnp.concatenate([jnp.cos(angle), -jnp.sin(angle)], axis=0).astype(jnp.bfloat16)


def _frame_kernel(v_ref, w_ref, o_ref):
    n = w_ref.shape[1]
    group = o_ref.shape[0]
    lhs = jnp.concatenate([v_ref[:, g * n : (g + 1) * n] for g in range(group)], axis=0)
    res = lax.dot_general(
        lhs, w_ref[...], (((1,), (1,)), ((), ())), preferred_element_type=jnp.float32
    )
    o_ref[...] = res.reshape(o_ref.shape)


def frame_products(voltages, weights, fft_length, group):
    rows, samples = voltages.shape
    frames = samples // fft_length
    steps = -(-frames // group)
    width = weights.shape[0]
    return pl.pallas_call(
        _frame_kernel,
        grid=(steps,),
        in_specs=[
            pl.BlockSpec((rows, group * fft_length), lambda f: (0, f)),
            pl.BlockSpec((width, fft_length), lambda f: (0, 0)),
        ],
        out_specs=pl.BlockSpec((group, rows, width), lambda f: (f, 0, 0)),
        out_shape=jax.ShapeDtypeStruct((steps * group, rows, width), jnp.float32),
        compiler_params=pltpu.CompilerParams(vmem_limit_bytes=56 * 1024 * 1024),
    )(voltages, weights)


def channelize(voltages, filter_taps, channel_index):
    tap_count, fft_length = filter_taps.shape
    frame_count = voltages.shape[1] // fft_length
    spectra = frame_count - tap_count + 1
    twiddle = phase_table_t(channel_index, fft_length).astype(jnp.float32)
    cols = twiddle.shape[0]
    weights = (filter_taps[:, None, :] * twiddle[None, :, :]).astype(jnp.bfloat16)
    weights = weights.reshape(tap_count * cols, fft_length)
    prod = frame_products(voltages, weights, fft_length, 4)
    spec = prod[0:spectra, :, 0:cols]
    for m in range(1, tap_count):
        spec = spec + prod[m : m + spectra, :, m * cols : (m + 1) * cols]
    return spec


def slot_index(antenna_slot_order):
    count = antenna_slot_order.shape[0]
    ids = jnp.arange(count, dtype=jnp.int32)
    return jnp.sum(
        jnp.where(antenna_slot_order[None, :] == ids[:, None], ids[None, :], 0), axis=1
    )


def split2(x):
    hi = x.astype(jnp.bfloat16)
    lo = (x - hi.astype(jnp.float32)).astype(jnp.bfloat16)
    return hi, lo


def _corr_kernel(l_ref, o_ref, out_ref):
    res = jnp.dot(l_ref[0], o_ref[0], preferred_element_type=jnp.float32)
    out_ref[0] = res.astype(out_ref.dtype).reshape(out_ref.shape[1:])


def correlate(lhs, rhs, block_rows):
    chans, slots, pairs, width = lhs.shape
    cols = rhs.shape[2]
    lhs = lhs.reshape(chans, slots * pairs, width)
    return pl.pallas_call(
        _corr_kernel,
        grid=(chans, slots // block_rows),
        in_specs=[
            pl.BlockSpec((1, block_rows * pairs, width), lambda c, s: (c, s, 0)),
            pl.BlockSpec((1, width, cols), lambda c, s: (c, 0, 0)),
        ],
        out_specs=pl.BlockSpec((1, block_rows, pairs, cols), lambda c, s: (c, s, 0, 0)),
        out_shape=jax.ShapeDtypeStruct((chans, slots, pairs, cols), jnp.bfloat16),
        compiler_params=pltpu.CompilerParams(vmem_limit_bytes=48 * 1024 * 1024),
    )(lhs, rhs)


def per_device(voltages, filter_taps, channel_index, antenna_slot_order):
    spec = channelize(voltages, filter_taps, channel_index)
    spectra, rows, cols = spec.shape
    chans = cols // 2
    grp = lax.psum(1, "grp")
    local_ch = chans // grp
    x = spec.reshape(spectra, rows, 2, chans).transpose(1, 3, 2, 0)
    x = lax.all_to_all(x, "grp", split_axis=1, concat_axis=0, tiled=True)
    slots_local = x.shape[0]
    x = x.reshape(slots_local, local_ch * 2 * spectra)
    everything = lax.all_gather(x, "blk", axis=0, tiled=True)
    inverse = slot_index(antenna_slot_order)
    width = everything.shape[1]
    ordered = jnp.take(everything.reshape(-1, 2 * width), inverse, axis=0)
    ordered = ordered.reshape(-1, width)
    ordered = ordered.reshape(-1, local_ch, 2 * spectra).transpose(1, 0, 2)
    scale = jnp.float32(1.0 / spectra)
    xl = x.reshape(slots_local, local_ch, 2, spectra).transpose(1, 0, 2, 3) * scale
    re = xl[:, :, 0, :]
    im = xl[:, :, 1, :]
    row0 = jnp.concatenate([re, im], axis=-1)
    row1 = jnp.concatenate([im, -re], axis=-1)
    lhs = jnp.stack([row0, row1], axis=2)
    la, lb = split2(lhs)
    o1, o2 = split2(ordered)
    lcat = jnp.concatenate([la, la, lb], axis=-1)
    rhs = jnp.concatenate([o1, o2, o1], axis=-1).transpose(0, 2, 1)
    result = correlate(lcat, rhs, min(128, slots_local))
    return result


def solution(mesh):
    in_specs = (P(("blk", "grp"), None), P(), P(), P())
    out_specs = P("grp", "blk", None, None)
    return jax.shard_map(
        per_device, mesh=mesh, in_specs=in_specs, out_specs=out_specs, check_vma=False
    )
```

```python
import math

import jax
import jax.numpy as jnp
from jax import lax
from jax.experimental import pallas as pl
from jax.experimental.pallas import tpu as pltpu
from jax.sharding import PartitionSpec as P


def phase_table(channel_index, fft_length):
    samples_idx = jnp.arange(fft_length, dtype=jnp.int32)
    phase = samples_idx[:, None] * channel_index[None, :] % fft_length
    angle = phase.astype(jnp.float32) * jnp.float32(2.0 * math.pi / fft_length)
    return jnp.concatenate([jnp.cos(angle), -jnp.sin(angle)], axis=1).astype(jnp.bfloat16)


def phase_table_t(channel_index, fft_length):
    samples_idx = jnp.arange(fft_length, dtype=jnp.int32)
    phase = channel_index[:, None] * samples_idx[None, :] % fft_length
    angle = phase.astype(jnp.float32) * jnp.float32(2.0 * math.pi / fft_length)
    return jnp.concatenate([jnp.cos(angle), -jnp.sin(angle)], axis=0).astype(jnp.bfloat16)


def _frame_kernel(v_ref, w_ref, o_ref):
    n = w_ref.shape[1]
    group = o_ref.shape[0]
    lhs = jnp.concatenate([v_ref[:, g * n : (g + 1) * n] for g in range(group)], axis=0)
    res = lax.dot_general(
        lhs, w_ref[...], (((1,), (1,)), ((), ())), preferred_element_type=jnp.float32
    )
    o_ref[...] = res.reshape(o_ref.shape)


def frame_products(voltages, weights, fft_length, group):
    rows, samples = voltages.shape
    frames = samples // fft_length
    steps = -(-frames // group)
    width = weights.shape[0]
    return pl.pallas_call(
        _frame_kernel,
        grid=(steps,),
        in_specs=[
            pl.BlockSpec((rows, group * fft_length), lambda f: (0, f)),
            pl.BlockSpec((width, fft_length), lambda f: (0, 0)),
        ],
        out_specs=pl.BlockSpec((group, rows, width), lambda f: (f, 0, 0)),
        out_shape=jax.ShapeDtypeStruct((steps * group, rows, width), jnp.float32),
        compiler_params=pltpu.CompilerParams(vmem_limit_bytes=56 * 1024 * 1024),
    )(voltages, weights)


def channelize(voltages, filter_taps, channel_index):
    tap_count, fft_length = filter_taps.shape
    frame_count = voltages.shape[1] // fft_length
    spectra = frame_count - tap_count + 1
    twiddle = phase_table_t(channel_index, fft_length).astype(jnp.float32)
    cols = twiddle.shape[0]
    weights = (filter_taps[:, None, :] * twiddle[None, :, :]).astype(jnp.bfloat16)
    weights = weights.reshape(tap_count * cols, fft_length)
    prod = frame_products(voltages, weights, fft_length, 4)
    spec = prod[0:spectra, :, 0:cols]
    for m in range(1, tap_count):
        spec = spec + prod[m : m + spectra, :, m * cols : (m + 1) * cols]
    return spec


def slot_index(antenna_slot_order):
    count = antenna_slot_order.shape[0]
    ids = jnp.arange(count, dtype=jnp.int32)
    return jnp.sum(
        jnp.where(antenna_slot_order[None, :] == ids[:, None], ids[None, :], 0), axis=1
    )


def _perm_kernel(inv_ref, e_ref, o_ref):
    def body(a, carry):
        src = inv_ref[a] * 2
        o_ref[pl.ds(2 * a, 2), :] = e_ref[pl.ds(src, 2), :]
        return carry

    lax.fori_loop(0, inv_ref.shape[0], body, 0, unroll=8)


def permute_pairs(everything, inverse):
    rows, width = everything.shape
    return pl.pallas_call(
        _perm_kernel,
        grid_spec=pltpu.PrefetchScalarGridSpec(
            num_scalar_prefetch=1,
            grid=(1,),
            in_specs=[pl.BlockSpec((rows, width), lambda i, inv: (0, 0))],
            out_specs=pl.BlockSpec((rows, width), lambda i, inv: (0, 0)),
        ),
        out_shape=jax.ShapeDtypeStruct((rows, width), everything.dtype),
    )(inverse, everything)


def split2(x):
    hi = x.astype(jnp.bfloat16)
    lo = (x - hi.astype(jnp.float32)).astype(jnp.bfloat16)
    return hi, lo


def _corr_kernel(l_ref, o_ref, out_ref):
    res = jnp.dot(l_ref[0], o_ref[0], preferred_element_type=jnp.float32)
    out_ref[0] = res.astype(out_ref.dtype).reshape(out_ref.shape[1:])


def correlate(lhs, rhs, block_rows):
    chans, slots, pairs, width = lhs.shape
    cols = rhs.shape[2]
    lhs = lhs.reshape(chans, slots * pairs, width)
    return pl.pallas_call(
        _corr_kernel,
        grid=(chans, slots // block_rows),
        in_specs=[
            pl.BlockSpec((1, block_rows * pairs, width), lambda c, s: (c, s, 0)),
            pl.BlockSpec((1, width, cols), lambda c, s: (c, 0, 0)),
        ],
        out_specs=pl.BlockSpec((1, block_rows, pairs, cols), lambda c, s: (c, s, 0, 0)),
        out_shape=jax.ShapeDtypeStruct((chans, slots, pairs, cols), jnp.bfloat16),
        compiler_params=pltpu.CompilerParams(vmem_limit_bytes=48 * 1024 * 1024),
    )(lhs, rhs)


def per_device(voltages, filter_taps, channel_index, antenna_slot_order):
    spec = channelize(voltages, filter_taps, channel_index)
    spectra, rows, cols = spec.shape
    chans = cols // 2
    grp = lax.psum(1, "grp")
    local_ch = chans // grp
    x = spec.reshape(spectra, rows, 2, chans).transpose(1, 3, 2, 0)
    x = lax.all_to_all(x, "grp", split_axis=1, concat_axis=0, tiled=True)
    slots_local = x.shape[0]
    x = x.reshape(slots_local, local_ch * 2 * spectra)
    everything = lax.all_gather(x, "blk", axis=0, tiled=True)
    inverse = slot_index(antenna_slot_order)
    ordered = permute_pairs(everything, inverse)
    ordered = ordered.reshape(-1, local_ch, 2 * spectra).transpose(1, 0, 2)
    scale = jnp.float32(1.0 / spectra)
    xl = x.reshape(slots_local, local_ch, 2, spectra).transpose(1, 0, 2, 3) * scale
    re = xl[:, :, 0, :]
    im = xl[:, :, 1, :]
    row0 = jnp.concatenate([re, im], axis=-1)
    row1 = jnp.concatenate([im, -re], axis=-1)
    lhs = jnp.stack([row0, row1], axis=2)
    la, lb = split2(lhs)
    o1, o2 = split2(ordered)
    lcat = jnp.concatenate([la, la, lb], axis=-1)
    rhs = jnp.concatenate([o1, o2, o1], axis=-1).transpose(0, 2, 1)
    result = correlate(lcat, rhs, min(256, slots_local))
    return result


def solution(mesh):
    in_specs = (P(("blk", "grp"), None), P(), P(), P())
    out_specs = P("grp", "blk", None, None)
    return jax.shard_map(
        per_device, mesh=mesh, in_specs=in_specs, out_specs=out_specs, check_vma=False
    )
```

```python
import math

import jax
import jax.numpy as jnp
from jax import lax
from jax.experimental import pallas as pl
from jax.experimental.pallas import tpu as pltpu
from jax.sharding import PartitionSpec as P


def phase_table(channel_index, fft_length):
    samples_idx = jnp.arange(fft_length, dtype=jnp.int32)
    phase = samples_idx[:, None] * channel_index[None, :] % fft_length
    angle = phase.astype(jnp.float32) * jnp.float32(2.0 * math.pi / fft_length)
    return jnp.concatenate([jnp.cos(angle), -jnp.sin(angle)], axis=1).astype(jnp.bfloat16)


def phase_table_t(channel_index, fft_length):
    samples_idx = jnp.arange(fft_length, dtype=jnp.int32)
    phase = channel_index[:, None] * samples_idx[None, :] % fft_length
    angle = phase.astype(jnp.float32) * jnp.float32(2.0 * math.pi / fft_length)
    return jnp.concatenate([jnp.cos(angle), -jnp.sin(angle)], axis=0).astype(jnp.bfloat16)


def _frame_kernel(v_ref, w_ref, o_ref, p_ref):
    i = pl.program_id(0)
    n = w_ref.shape[1]
    spectra, rows, cols = o_ref.shape
    group = p_ref.shape[0] // pl.num_programs(0)
    lhs = jnp.concatenate([v_ref[:, g * n : (g + 1) * n] for g in range(group)], axis=0)
    res = lax.dot_general(
        lhs, w_ref[...], (((1,), (1,)), ((), ())), preferred_element_type=jnp.float32
    )
    p_ref[pl.ds(i * group, group)] = res.reshape(group, rows, res.shape[1])

    @pl.when(i == pl.num_programs(0) - 1)
    def _():
        taps = res.shape[1] // cols
        acc = p_ref[0:spectra, :, 0:cols]
        for m in range(1, taps):
            acc = acc + p_ref[m : m + spectra, :, m * cols : (m + 1) * cols]
        o_ref[...] = acc


def frame_products(voltages, weights, fft_length, group, spectra):
    rows, samples = voltages.shape
    frames = samples // fft_length
    steps = -(-frames // group)
    width, _ = weights.shape
    cols = width // (frames - spectra + 1)
    return pl.pallas_call(
        _frame_kernel,
        grid=(steps,),
        in_specs=[
            pl.BlockSpec((rows, group * fft_length), lambda f: (0, f)),
            pl.BlockSpec((width, fft_length), lambda f: (0, 0)),
        ],
        out_specs=pl.BlockSpec((spectra, rows, cols), lambda f: (0, 0, 0)),
        out_shape=jax.ShapeDtypeStruct((spectra, rows, cols), jnp.float32),
        scratch_shapes=[pltpu.VMEM((steps * group, rows, width), jnp.float32)],
        compiler_params=pltpu.CompilerParams(vmem_limit_bytes=56 * 1024 * 1024),
    )(voltages, weights)


def channelize(voltages, filter_taps, channel_index):
    tap_count, fft_length = filter_taps.shape
    frame_count = voltages.shape[1] // fft_length
    spectra = frame_count - tap_count + 1
    twiddle = phase_table_t(channel_index, fft_length).astype(jnp.float32)
    cols = twiddle.shape[0]
    weights = (filter_taps[:, None, :] * twiddle[None, :, :]).astype(jnp.bfloat16)
    weights = weights.reshape(tap_count * cols, fft_length)
    return frame_products(voltages, weights, fft_length, 4, spectra)


def slot_index(antenna_slot_order):
    count = antenna_slot_order.shape[0]
    ids = jnp.arange(count, dtype=jnp.int32)
    return jnp.sum(
        jnp.where(antenna_slot_order[None, :] == ids[:, None], ids[None, :], 0), axis=1
    )


def _perm_kernel(inv_ref, e_ref, o_ref):
    def body(a, carry):
        src = inv_ref[a] * 2
        o_ref[pl.ds(2 * a, 2), :] = e_ref[pl.ds(src, 2), :]
        return carry

    lax.fori_loop(0, inv_ref.shape[0], body, 0, unroll=8)


def permute_pairs(everything, inverse):
    rows, width = everything.shape
    return pl.pallas_call(
        _perm_kernel,
        grid_spec=pltpu.PrefetchScalarGridSpec(
            num_scalar_prefetch=1,
            grid=(1,),
            in_specs=[pl.BlockSpec((rows, width), lambda i, inv: (0, 0))],
            out_specs=pl.BlockSpec((rows, width), lambda i, inv: (0, 0)),
        ),
        out_shape=jax.ShapeDtypeStruct((rows, width), everything.dtype),
    )(inverse, everything)


def split2(x):
    hi = x.astype(jnp.bfloat16)
    lo = (x - hi.astype(jnp.float32)).astype(jnp.bfloat16)
    return hi, lo


def _corr_kernel(l_ref, o_ref, out_ref):
    res = jnp.dot(l_ref[0], o_ref[0], preferred_element_type=jnp.float32)
    out_ref[0] = res.astype(out_ref.dtype).reshape(out_ref.shape[1:])


def correlate(lhs, rhs, block_rows):
    chans, slots, pairs, width = lhs.shape
    cols = rhs.shape[2]
    lhs = lhs.reshape(chans, slots * pairs, width)
    return pl.pallas_call(
        _corr_kernel,
        grid=(chans, slots // block_rows),
        in_specs=[
            pl.BlockSpec((1, block_rows * pairs, width), lambda c, s: (c, s, 0)),
            pl.BlockSpec((1, width, cols), lambda c, s: (c, 0, 0)),
        ],
        out_specs=pl.BlockSpec((1, block_rows, pairs, cols), lambda c, s: (c, s, 0, 0)),
        out_shape=jax.ShapeDtypeStruct((chans, slots, pairs, cols), jnp.bfloat16),
        compiler_params=pltpu.CompilerParams(vmem_limit_bytes=48 * 1024 * 1024),
    )(lhs, rhs)


def exchange_channels(x, grp, local_ch):
    me = lax.axis_index("grp")
    got = []
    for d in range(grp):
        part = lax.dynamic_slice_in_dim(x, ((me + d) % grp) * local_ch, local_ch, axis=1)
        if d:
            part = lax.ppermute(part, "grp", [(j, (j + d) % grp) for j in range(grp)])
        got.append(part)
    stacked = jnp.stack(got, axis=0)
    order = (me - jnp.arange(grp, dtype=jnp.int32)) % grp
    stacked = jnp.take(stacked, order, axis=0)
    return stacked.reshape((grp * x.shape[0],) + stacked.shape[2:])


def per_device(voltages, filter_taps, channel_index, antenna_slot_order):
    spec = channelize(voltages, filter_taps, channel_index)
    spectra, rows, cols = spec.shape
    chans = cols // 2
    grp = lax.psum(1, "grp")
    local_ch = chans // grp
    x = spec.reshape(spectra, rows, 2, chans).transpose(1, 3, 2, 0)
    x = exchange_channels(x, grp, local_ch)
    slots_local = x.shape[0]
    x = x.reshape(slots_local, local_ch * 2 * spectra)
    everything = lax.all_gather(x, "blk", axis=0, tiled=True)
    inverse = slot_index(antenna_slot_order)
    ordered = permute_pairs(everything, inverse)
    ordered = ordered.reshape(-1, local_ch, 2 * spectra).transpose(1, 0, 2)
    scale = jnp.float32(1.0 / spectra)
    xl = x.reshape(slots_local, local_ch, 2, spectra).transpose(1, 0, 2, 3) * scale
    re = xl[:, :, 0, :]
    im = xl[:, :, 1, :]
    row0 = jnp.concatenate([re, im], axis=-1)
    row1 = jnp.concatenate([im, -re], axis=-1)
    lhs = jnp.stack([row0, row1], axis=2)
    la, lb = split2(lhs)
    o1, o2 = split2(ordered)
    lcat = jnp.concatenate([la, la, lb], axis=-1)
    rhs = jnp.concatenate([o1, o2, o1], axis=-1).transpose(0, 2, 1)
    result = correlate(lcat, rhs, min(256, slots_local))
    return result


def solution(mesh):
    in_specs = (P(("blk", "grp"), None), P(), P(), P())
    out_specs = P("grp", "blk", None, None)
    return jax.shard_map(
        per_device, mesh=mesh, in_specs=in_specs, out_specs=out_specs, check_vma=False
    )
```

```python
import functools
import math

import jax
import jax.numpy as jnp
from jax import lax
from jax.experimental import pallas as pl
from jax.experimental.pallas import tpu as pltpu
from jax.sharding import PartitionSpec as P


def phase_table(channel_index, fft_length):
    samples_idx = jnp.arange(fft_length, dtype=jnp.int32)
    phase = samples_idx[:, None] * channel_index[None, :] % fft_length
    angle = phase.astype(jnp.float32) * jnp.float32(2.0 * math.pi / fft_length)
    return jnp.concatenate([jnp.cos(angle), -jnp.sin(angle)], axis=1).astype(jnp.bfloat16)


def phase_table_t(channel_index, fft_length):
    samples_idx = jnp.arange(fft_length, dtype=jnp.int32)
    phase = channel_index[:, None] * samples_idx[None, :] % fft_length
    angle = phase.astype(jnp.float32) * jnp.float32(2.0 * math.pi / fft_length)
    return jnp.concatenate([jnp.cos(angle), -jnp.sin(angle)], axis=0).astype(jnp.bfloat16)


def _frame_kernel(v_ref, w_ref, o_ref, p_ref):
    i = pl.program_id(0)
    n = w_ref.shape[1]
    spectra, rows, cols = o_ref.shape
    group = p_ref.shape[0] // pl.num_programs(0)
    lhs = jnp.concatenate([v_ref[:, g * n : (g + 1) * n] for g in range(group)], axis=0)
    res = lax.dot_general(
        lhs, w_ref[...], (((1,), (1,)), ((), ())), preferred_element_type=jnp.float32
    )
    p_ref[pl.ds(i * group, group)] = res.reshape(group, rows, res.shape[1])

    @pl.when(i == pl.num_programs(0) - 1)
    def _():
        taps = res.shape[1] // cols
        acc = p_ref[0:spectra, :, 0:cols]
        for m in range(1, taps):
            acc = acc + p_ref[m : m + spectra, :, m * cols : (m + 1) * cols]
        o_ref[...] = acc


def frame_products(voltages, weights, fft_length, group, spectra, part, parts):
    rows, samples = voltages.shape
    rows = rows // parts
    frames = samples // fft_length
    steps = -(-frames // group)
    width, _ = weights.shape
    cols = width // (frames - spectra + 1)
    return pl.pallas_call(
        _frame_kernel,
        grid=(steps,),
        in_specs=[
            pl.BlockSpec((rows, group * fft_length), lambda f: (part, f)),
            pl.BlockSpec((width, fft_length), lambda f: (0, 0)),
        ],
        out_specs=pl.BlockSpec((spectra, rows, cols), lambda f: (0, 0, 0)),
        out_shape=jax.ShapeDtypeStruct((spectra, rows, cols), jnp.float32),
        scratch_shapes=[pltpu.VMEM((steps * group, rows, width), jnp.float32)],
        compiler_params=pltpu.CompilerParams(vmem_limit_bytes=56 * 1024 * 1024),
    )(voltages, weights)


def tap_weights(filter_taps, channel_index):
    tap_count, fft_length = filter_taps.shape
    twiddle = phase_table_t(channel_index, fft_length).astype(jnp.float32)
    cols = twiddle.shape[0]
    weights = (filter_taps[:, None, :] * twiddle[None, :, :]).astype(jnp.bfloat16)
    return weights.reshape(tap_count * cols, fft_length)


def slot_index(antenna_slot_order):
    count = antenna_slot_order.shape[0]
    ids = jnp.arange(count, dtype=jnp.int32)
    return jnp.sum(
        jnp.where(antenna_slot_order[None, :] == ids[:, None], ids[None, :], 0), axis=1
    )


def _perm_kernel(part_rows, inv_ref, *refs):
    srcs, o_ref = refs[:-1], refs[-1]
    parts = len(srcs)

    def body(a, carry):
        u = inv_ref[a] * 2
        h = (u // part_rows) % parts
        row = (u // (parts * part_rows)) * part_rows + u % part_rows
        val = srcs[0][pl.ds(row, 2), :]
        for k in range(1, parts):
            val = jnp.where(h == k, srcs[k][pl.ds(row, 2), :], val)
        o_ref[pl.ds(2 * a, 2), :] = val
        return carry

    lax.fori_loop(0, inv_ref.shape[0], body, 0, unroll=8)


def permute_pairs(parts_list, inverse, part_rows):
    rows, width = parts_list[0].shape
    total = rows * len(parts_list)
    spec = pl.BlockSpec((rows, width), lambda i, inv: (0, 0))
    return pl.pallas_call(
        functools.partial(_perm_kernel, part_rows),
        grid_spec=pltpu.PrefetchScalarGridSpec(
            num_scalar_prefetch=1,
            grid=(1,),
            in_specs=[spec] * len(parts_list),
            out_specs=pl.BlockSpec((total, width), lambda i, inv: (0, 0)),
        ),
        out_shape=jax.ShapeDtypeStruct((total, width), parts_list[0].dtype),
    )(inverse, *parts_list)


def split2(x):
    hi = x.astype(jnp.bfloat16)
    lo = (x - hi.astype(jnp.float32)).astype(jnp.bfloat16)
    return hi, lo


def _corr_kernel(l_ref, o_ref, out_ref):
    res = jnp.dot(l_ref[0], o_ref[0], preferred_element_type=jnp.float32)
    out_ref[0] = res.astype(out_ref.dtype).reshape(out_ref.shape[1:])


def correlate(lhs, rhs, block_rows):
    chans, slots, pairs, width = lhs.shape
    cols = rhs.shape[2]
    lhs = lhs.reshape(chans, slots * pairs, width)
    return pl.pallas_call(
        _corr_kernel,
        grid=(chans, slots // block_rows),
        in_specs=[
            pl.BlockSpec((1, block_rows * pairs, width), lambda c, s: (c, s, 0)),
            pl.BlockSpec((1, width, cols), lambda c, s: (c, 0, 0)),
        ],
        out_specs=pl.BlockSpec((1, block_rows, pairs, cols), lambda c, s: (c, s, 0, 0)),
        out_shape=jax.ShapeDtypeStruct((chans, slots, pairs, cols), jnp.bfloat16),
        compiler_params=pltpu.CompilerParams(vmem_limit_bytes=48 * 1024 * 1024),
    )(lhs, rhs)


def exchange_channels(x, grp, local_ch):
    me = lax.axis_index("grp")
    got = []
    for d in range(grp):
        part = lax.dynamic_slice_in_dim(x, ((me + d) % grp) * local_ch, local_ch, axis=1)
        if d:
            part = lax.ppermute(part, "grp", [(j, (j + d) % grp) for j in range(grp)])
        got.append(part)
    stacked = jnp.stack(got, axis=0)
    order = (me - jnp.arange(grp, dtype=jnp.int32)) % grp
    stacked = jnp.take(stacked, order, axis=0)
    return stacked.reshape((grp * x.shape[0],) + stacked.shape[2:])


def per_device(voltages, filter_taps, channel_index, antenna_slot_order):
    rows = voltages.shape[0]
    parts = 2 if rows % 32 == 0 else 1
    weights = tap_weights(filter_taps, channel_index)
    tap_count, fft_length = filter_taps.shape
    spectra = voltages.shape[1] // fft_length - tap_count + 1
    grp = lax.psum(1, "grp")
    locals_, gathered = [], []
    for h in range(parts):
        spec = frame_products(voltages, weights, fft_length, 4, spectra, h, parts)
        _, part_rows, cols = spec.shape
        chans = cols // 2
        local_ch = chans // grp
        x = spec.reshape(spectra, part_rows, 2, chans).transpose(1, 3, 2, 0)
        x = exchange_channels(x, grp, local_ch)
        x = x.reshape(grp, part_rows, local_ch * 2 * spectra)
        locals_.append(x)
        send = x.reshape(grp * part_rows, -1)
        voltages, send = lax.optimization_barrier((voltages, send))
        gathered.append(lax.all_gather(send, "blk", axis=0, tiled=True))
    x = jnp.stack(locals_, axis=1)
    slots_local = grp * parts * part_rows
    x = x.reshape(slots_local, local_ch * 2 * spectra)
    inverse = slot_index(antenna_slot_order)
    ordered = permute_pairs(gathered, inverse, part_rows)
    ordered = ordered.reshape(-1, local_ch, 2 * spectra).transpose(1, 0, 2)
    scale = jnp.float32(1.0 / spectra)
    xl = x.reshape(slots_local, local_ch, 2, spectra).transpose(1, 0, 2, 3) * scale
    re = xl[:, :, 0, :]
    im = xl[:, :, 1, :]
    row0 = jnp.concatenate([re, im], axis=-1)
    row1 = jnp.concatenate([im, -re], axis=-1)
    lhs = jnp.stack([row0, row1], axis=2)
    la, lb = split2(lhs)
    o1, o2 = split2(ordered)
    lcat = jnp.concatenate([la, la, lb], axis=-1)
    rhs = jnp.concatenate([o1, o2, o1], axis=-1).transpose(0, 2, 1)
    result = correlate(lcat, rhs, min(256, slots_local))
    return result


def solution(mesh):
    in_specs = (P(("blk", "grp"), None), P(), P(), P())
    out_specs = P("grp", "blk", None, None)
    return jax.shard_map(
        per_device, mesh=mesh, in_specs=in_specs, out_specs=out_specs, check_vma=False
    )
```

```python
import functools
import math

import jax
import jax.numpy as jnp
from jax import lax
from jax.experimental import pallas as pl
from jax.experimental.pallas import tpu as pltpu
from jax.sharding import PartitionSpec as P


def phase_table(channel_index, fft_length):
    samples_idx = jnp.arange(fft_length, dtype=jnp.int32)
    phase = samples_idx[:, None] * channel_index[None, :] % fft_length
    angle = phase.astype(jnp.float32) * jnp.float32(2.0 * math.pi / fft_length)
    return jnp.concatenate([jnp.cos(angle), -jnp.sin(angle)], axis=1).astype(jnp.bfloat16)


def phase_table_t(channel_index, fft_length):
    samples_idx = jnp.arange(fft_length, dtype=jnp.int32)
    phase = channel_index[:, None] * samples_idx[None, :] % fft_length
    angle = phase.astype(jnp.float32) * jnp.float32(2.0 * math.pi / fft_length)
    return jnp.concatenate([jnp.cos(angle), -jnp.sin(angle)], axis=0).astype(jnp.bfloat16)


def _frame_kernel(chunk, v_hbm, w_ref, o_ref, buf, acc, sem):
    spectra, rows, cols = o_ref.shape
    width, n = w_ref.shape
    frames = buf.shape[1] // rows
    chunks = n // chunk

    def copies(k, slot):
        return [
            pltpu.make_async_copy(
                v_hbm.at[:, pl.ds(f * n + k * chunk, chunk)],
                buf.at[slot, pl.ds(f * rows, rows), :],
                sem.at[slot, f],
            )
            for f in range(frames)
        ]

    for c in copies(0, 0):
        c.start()
    acc[...] = jnp.zeros(acc.shape, acc.dtype)

    def step(k, carry):
        slot = k % 2

        @pl.when(k + 1 < chunks)
        def _():
            for c in copies(k + 1, 1 - slot):
                c.start()

        for c in copies(k, slot):
            c.wait()
        start = pl.multiple_of(k * chunk, chunk)
        acc[...] += lax.dot_general(
            buf[slot],
            w_ref[:, pl.ds(start, chunk)],
            (((1,), (1,)), ((), ())),
            preferred_element_type=jnp.float32,
        )
        return carry

    lax.fori_loop(0, chunks, step, 0)
    taps = width // cols
    total = acc[...].reshape(frames, rows, width)
    out = total[0:spectra, :, 0:cols]
    for m in range(1, taps):
        out = out + total[m : m + spectra, :, m * cols : (m + 1) * cols]
    o_ref[...] = out


def frame_products(voltages, weights, fft_length, spectra):
    rows, samples = voltages.shape
    frames = samples // fft_length
    width, _ = weights.shape
    cols = width // (frames - spectra + 1)
    chunk = 1024
    return pl.pallas_call(
        functools.partial(_frame_kernel, chunk),
        in_specs=[
            pl.BlockSpec(memory_space=pl.ANY),
            pl.BlockSpec(memory_space=pltpu.VMEM),
        ],
        out_specs=pl.BlockSpec(memory_space=pltpu.VMEM),
        out_shape=jax.ShapeDtypeStruct((spectra, rows, cols), jnp.float32),
        scratch_shapes=[
            pltpu.VMEM((2, frames * rows, chunk), voltages.dtype),
            pltpu.VMEM((frames * rows, width), jnp.float32),
            pltpu.SemaphoreType.DMA((2, frames)),
        ],
        compiler_params=pltpu.CompilerParams(vmem_limit_bytes=60 * 1024 * 1024),
    )(voltages, weights)


def channelize(voltages, filter_taps, channel_index):
    tap_count, fft_length = filter_taps.shape
    frame_count = voltages.shape[1] // fft_length
    spectra = frame_count - tap_count + 1
    twiddle = phase_table_t(channel_index, fft_length).astype(jnp.float32)
    cols = twiddle.shape[0]
    weights = (filter_taps[:, None, :] * twiddle[None, :, :]).astype(jnp.bfloat16)
    weights = weights.reshape(tap_count * cols, fft_length)
    return frame_products(voltages, weights, fft_length, spectra)


def slot_index(antenna_slot_order):
    count = antenna_slot_order.shape[0]
    ids = jnp.arange(count, dtype=jnp.int32)
    return jnp.sum(
        jnp.where(antenna_slot_order[None, :] == ids[:, None], ids[None, :], 0), axis=1
    )


def _perm_kernel(inv_ref, e_ref, o_ref):
    def body(a, carry):
        src = inv_ref[a] * 2
        o_ref[pl.ds(2 * a, 2), :] = e_ref[pl.ds(src, 2), :]
        return carry

    lax.fori_loop(0, inv_ref.shape[0], body, 0, unroll=8)


def permute_pairs(everything, inverse):
    rows, width = everything.shape
    return pl.pallas_call(
        _perm_kernel,
        grid_spec=pltpu.PrefetchScalarGridSpec(
            num_scalar_prefetch=1,
            grid=(1,),
            in_specs=[pl.BlockSpec((rows, width), lambda i, inv: (0, 0))],
            out_specs=pl.BlockSpec((rows, width), lambda i, inv: (0, 0)),
        ),
        out_shape=jax.ShapeDtypeStruct((rows, width), everything.dtype),
    )(inverse, everything)


def split2(x):
    hi = x.astype(jnp.bfloat16)
    lo = (x - hi.astype(jnp.float32)).astype(jnp.bfloat16)
    return hi, lo


def _corr_kernel(l_ref, o_ref, out_ref):
    res = jnp.dot(l_ref[0], o_ref[0], preferred_element_type=jnp.float32)
    out_ref[0] = res.astype(out_ref.dtype).reshape(out_ref.shape[1:])


def correlate(lhs, rhs, block_rows):
    chans, slots, pairs, width = lhs.shape
    cols = rhs.shape[2]
    lhs = lhs.reshape(chans, slots * pairs, width)
    return pl.pallas_call(
        _corr_kernel,
        grid=(chans, slots // block_rows),
        in_specs=[
            pl.BlockSpec((1, block_rows * pairs, width), lambda c, s: (c, s, 0)),
            pl.BlockSpec((1, width, cols), lambda c, s: (c, 0, 0)),
        ],
        out_specs=pl.BlockSpec((1, block_rows, pairs, cols), lambda c, s: (c, s, 0, 0)),
        out_shape=jax.ShapeDtypeStruct((chans, slots, pairs, cols), jnp.bfloat16),
        compiler_params=pltpu.CompilerParams(vmem_limit_bytes=48 * 1024 * 1024),
    )(lhs, rhs)


def exchange_channels(x, grp, local_ch):
    me = lax.axis_index("grp")
    got = []
    for d in range(grp):
        part = lax.dynamic_slice_in_dim(x, ((me + d) % grp) * local_ch, local_ch, axis=1)
        if d:
            part = lax.ppermute(part, "grp", [(j, (j + d) % grp) for j in range(grp)])
        got.append(part)
    stacked = jnp.stack(got, axis=0)
    order = (me - jnp.arange(grp, dtype=jnp.int32)) % grp
    stacked = jnp.take(stacked, order, axis=0)
    return stacked.reshape((grp * x.shape[0],) + stacked.shape[2:])


def per_device(voltages, filter_taps, channel_index, antenna_slot_order):
    spec = channelize(voltages, filter_taps, channel_index)
    spectra, rows, cols = spec.shape
    chans = cols // 2
    grp = lax.psum(1, "grp")
    local_ch = chans // grp
    x = spec.reshape(spectra, rows, 2, chans).transpose(1, 3, 2, 0)
    x = exchange_channels(x, grp, local_ch)
    slots_local = x.shape[0]
    x = x.reshape(slots_local, local_ch * 2 * spectra)
    everything = lax.all_gather(x, "blk", axis=0, tiled=True)
    inverse = slot_index(antenna_slot_order)
    ordered = permute_pairs(everything, inverse)
    ordered = ordered.reshape(-1, local_ch, 2 * spectra).transpose(1, 0, 2)
    scale = jnp.float32(1.0 / spectra)
    xl = x.reshape(slots_local, local_ch, 2, spectra).transpose(1, 0, 2, 3) * scale
    re = xl[:, :, 0, :]
    im = xl[:, :, 1, :]
    row0 = jnp.concatenate([re, im], axis=-1)
    row1 = jnp.concatenate([im, -re], axis=-1)
    lhs = jnp.stack([row0, row1], axis=2)
    la, lb = split2(lhs)
    o1, o2 = split2(ordered)
    lcat = jnp.concatenate([la, la, lb], axis=-1)
    rhs = jnp.concatenate([o1, o2, o1], axis=-1).transpose(0, 2, 1)
    result = correlate(lcat, rhs, min(256, slots_local))
    return result


def solution(mesh):
    in_specs = (P(("blk", "grp"), None), P(), P(), P())
    out_specs = P("grp", "blk", None, None)
    return jax.shard_map(
        per_device, mesh=mesh, in_specs=in_specs, out_specs=out_specs, check_vma=False
    )
```

```python
import math

import jax
import jax.numpy as jnp
from jax import lax
from jax.experimental import pallas as pl
from jax.experimental.pallas import tpu as pltpu
from jax.sharding import PartitionSpec as P


def phase_table(channel_index, fft_length):
    samples_idx = jnp.arange(fft_length, dtype=jnp.int32)
    phase = samples_idx[:, None] * channel_index[None, :] % fft_length
    angle = phase.astype(jnp.float32) * jnp.float32(2.0 * math.pi / fft_length)
    return jnp.concatenate([jnp.cos(angle), -jnp.sin(angle)], axis=1).astype(jnp.bfloat16)


def phase_table_t(channel_index, fft_length):
    samples_idx = jnp.arange(fft_length, dtype=jnp.int32)
    phase = channel_index[:, None] * samples_idx[None, :] % fft_length
    angle = phase.astype(jnp.float32) * jnp.float32(2.0 * math.pi / fft_length)
    return jnp.concatenate([jnp.cos(angle), -jnp.sin(angle)], axis=0).astype(jnp.bfloat16)


def _frame_kernel(v_ref, w_ref, o_ref, p_ref):
    i = pl.program_id(0)
    n = w_ref.shape[1]
    spectra, rows, cols = o_ref.shape
    group = p_ref.shape[0] // pl.num_programs(0)
    lhs = jnp.concatenate([v_ref[:, g * n : (g + 1) * n] for g in range(group)], axis=0)
    res = lax.dot_general(
        lhs, w_ref[...], (((1,), (1,)), ((), ())), preferred_element_type=jnp.float32
    )
    p_ref[pl.ds(i * group, group)] = res.reshape(group, rows, res.shape[1])

    @pl.when(i == pl.num_programs(0) - 1)
    def _():
        taps = res.shape[1] // cols
        acc = p_ref[0:spectra, :, 0:cols]
        for m in range(1, taps):
            acc = acc + p_ref[m : m + spectra, :, m * cols : (m + 1) * cols]
        o_ref[...] = acc


def frame_products(voltages, weights, fft_length, group, spectra):
    rows, samples = voltages.shape
    frames = samples // fft_length
    steps = -(-frames // group)
    width, _ = weights.shape
    cols = width // (frames - spectra + 1)
    return pl.pallas_call(
        _frame_kernel,
        grid=(steps,),
        in_specs=[
            pl.BlockSpec((rows, group * fft_length), lambda f: (0, f)),
            pl.BlockSpec((width, fft_length), lambda f: (0, 0)),
        ],
        out_specs=pl.BlockSpec((spectra, rows, cols), lambda f: (0, 0, 0)),
        out_shape=jax.ShapeDtypeStruct((spectra, rows, cols), jnp.float32),
        scratch_shapes=[pltpu.VMEM((steps * group, rows, width), jnp.float32)],
        compiler_params=pltpu.CompilerParams(vmem_limit_bytes=56 * 1024 * 1024),
    )(voltages, weights)


def channelize(voltages, filter_taps, channel_index):
    tap_count, fft_length = filter_taps.shape
    frame_count = voltages.shape[1] // fft_length
    spectra = frame_count - tap_count + 1
    twiddle = phase_table_t(channel_index, fft_length).astype(jnp.float32)
    cols = twiddle.shape[0]
    weights = (filter_taps[:, None, :] * twiddle[None, :, :]).astype(jnp.bfloat16)
    weights = weights.reshape(tap_count * cols, fft_length)
    return frame_products(voltages, weights, fft_length, 4, spectra)


def slot_index(antenna_slot_order):
    count = antenna_slot_order.shape[0]
    ids = jnp.arange(count, dtype=jnp.int32)
    return jnp.sum(
        jnp.where(antenna_slot_order[None, :] == ids[:, None], ids[None, :], 0), axis=1
    )


def _perm_kernel(inv_ref, e_ref, o_ref):
    def body(a, carry):
        src = inv_ref[a] * 2
        o_ref[pl.ds(2 * a, 2), :] = e_ref[pl.ds(src, 2), :]
        return carry

    lax.fori_loop(0, inv_ref.shape[0], body, 0, unroll=8)


def permute_pairs(everything, inverse):
    rows, width = everything.shape
    return pl.pallas_call(
        _perm_kernel,
        grid_spec=pltpu.PrefetchScalarGridSpec(
            num_scalar_prefetch=1,
            grid=(1,),
            in_specs=[pl.BlockSpec((rows, width), lambda i, inv: (0, 0))],
            out_specs=pl.BlockSpec((rows, width), lambda i, inv: (0, 0)),
        ),
        out_shape=jax.ShapeDtypeStruct((rows, width), everything.dtype),
    )(inverse, everything)


def split2(x):
    hi = x.astype(jnp.bfloat16)
    lo = (x - hi.astype(jnp.float32)).astype(jnp.bfloat16)
    return hi, lo


def _corr_kernel(l_ref, o_ref, out_ref):
    res = jnp.dot(l_ref[0], o_ref[0], preferred_element_type=jnp.float32)
    out_ref[0] = res.astype(out_ref.dtype).reshape(out_ref.shape[1:])


def correlate(lhs, rhs, block_rows):
    chans, slots, pairs, width = lhs.shape
    cols = rhs.shape[2]
    lhs = lhs.reshape(chans, slots * pairs, width)
    return pl.pallas_call(
        _corr_kernel,
        grid=(chans, slots // block_rows),
        in_specs=[
            pl.BlockSpec((1, block_rows * pairs, width), lambda c, s: (c, s, 0)),
            pl.BlockSpec((1, width, cols), lambda c, s: (c, 0, 0)),
        ],
        out_specs=pl.BlockSpec((1, block_rows, pairs, cols), lambda c, s: (c, s, 0, 0)),
        out_shape=jax.ShapeDtypeStruct((chans, slots, pairs, cols), jnp.bfloat16),
        compiler_params=pltpu.CompilerParams(vmem_limit_bytes=48 * 1024 * 1024),
    )(lhs, rhs)


def exchange_channels(x, grp, local_ch):
    me = lax.axis_index("grp")
    got = []
    for d in range(grp):
        part = lax.dynamic_slice_in_dim(x, ((me + d) % grp) * local_ch, local_ch, axis=1)
        if d:
            part = lax.ppermute(part, "grp", [(j, (j + d) % grp) for j in range(grp)])
        got.append(part)
    stacked = jnp.stack(got, axis=0)
    order = (me - jnp.arange(grp, dtype=jnp.int32)) % grp
    stacked = jnp.take(stacked, order, axis=0)
    return stacked.reshape((grp * x.shape[0],) + stacked.shape[2:])


def gather_blocks(x):
    count = lax.psum(1, "blk")
    line = count // 2
    me = lax.axis_index("blk")
    pos, core = me // 2, me % 2
    right = [(z * 2 + c, (z + 1) * 2 + c) for z in range(line - 1) for c in range(2)]
    left = [(z * 2 + c, (z - 1) * 2 + c) for z in range(1, line) for c in range(2)]
    got_r, got_l = [], []
    r = x
    l = x
    for _ in range(1, line):
        r = lax.ppermute(r, "blk", right)
        l = lax.ppermute(l, "blk", left)
        got_r.append(r)
        got_l.append(l)
    cands = jnp.stack([x] + got_r + got_l, axis=0)
    zs = jnp.arange(line, dtype=jnp.int32)
    idx = jnp.where(zs == pos, 0, jnp.where(zs < pos, pos - zs, line - 1 + zs - pos))
    mine = jnp.take(cands, idx, axis=0)
    other = lax.ppermute(mine, "blk", [(b, b ^ 1) for b in range(count)])
    pair = jnp.where(core == 0, jnp.stack([mine, other], 1), jnp.stack([other, mine], 1))
    return pair.reshape((count * x.shape[0],) + x.shape[1:])


def per_device(voltages, filter_taps, channel_index, antenna_slot_order):
    spec = channelize(voltages, filter_taps, channel_index)
    spectra, rows, cols = spec.shape
    chans = cols // 2
    grp = lax.psum(1, "grp")
    local_ch = chans // grp
    x = spec.reshape(spectra, rows, 2, chans).transpose(1, 3, 2, 0)
    x = exchange_channels(x, grp, local_ch)
    slots_local = x.shape[0]
    x = x.reshape(slots_local, local_ch * 2 * spectra)
    everything = gather_blocks(x)
    inverse = slot_index(antenna_slot_order)
    ordered = permute_pairs(everything, inverse)
    ordered = ordered.reshape(-1, local_ch, 2 * spectra).transpose(1, 0, 2)
    scale = jnp.float32(1.0 / spectra)
    xl = x.reshape(slots_local, local_ch, 2, spectra).transpose(1, 0, 2, 3) * scale
    re = xl[:, :, 0, :]
    im = xl[:, :, 1, :]
    row0 = jnp.concatenate([re, im], axis=-1)
    row1 = jnp.concatenate([im, -re], axis=-1)
    lhs = jnp.stack([row0, row1], axis=2)
    la, lb = split2(lhs)
    o1, o2 = split2(ordered)
    lcat = jnp.concatenate([la, la, lb], axis=-1)
    rhs = jnp.concatenate([o1, o2, o1], axis=-1).transpose(0, 2, 1)
    result = correlate(lcat, rhs, min(256, slots_local))
    return result


def solution(mesh):
    in_specs = (P(("blk", "grp"), None), P(), P(), P())
    out_specs = P("grp", "blk", None, None)
    return jax.shard_map(
        per_device, mesh=mesh, in_specs=in_specs, out_specs=out_specs, check_vma=False
    )
```

```python
import math

import jax
import jax.numpy as jnp
from jax import lax
from jax.experimental import pallas as pl
from jax.experimental.pallas import tpu as pltpu
from jax.sharding import PartitionSpec as P


def phase_table(channel_index, fft_length):
    samples_idx = jnp.arange(fft_length, dtype=jnp.int32)
    phase = samples_idx[:, None] * channel_index[None, :] % fft_length
    angle = phase.astype(jnp.float32) * jnp.float32(2.0 * math.pi / fft_length)
    return jnp.concatenate([jnp.cos(angle), -jnp.sin(angle)], axis=1).astype(jnp.bfloat16)


def phase_table_t(channel_index, fft_length):
    samples_idx = jnp.arange(fft_length, dtype=jnp.int32)
    phase = channel_index[:, None] * samples_idx[None, :] % fft_length
    angle = phase.astype(jnp.float32) * jnp.float32(2.0 * math.pi / fft_length)
    return jnp.concatenate([jnp.cos(angle), -jnp.sin(angle)], axis=0).astype(jnp.bfloat16)


def _frame_kernel(v_ref, w_ref, o_ref, p_ref):
    i = pl.program_id(0)
    n = w_ref.shape[1]
    spectra, rows, cols = o_ref.shape
    group = p_ref.shape[0] // pl.num_programs(0)
    lhs = jnp.concatenate([v_ref[:, g * n : (g + 1) * n] for g in range(group)], axis=0)
    res = lax.dot_general(
        lhs, w_ref[...], (((1,), (1,)), ((), ())), preferred_element_type=jnp.float32
    )
    p_ref[pl.ds(i * group, group)] = res.reshape(group, rows, res.shape[1])

    @pl.when(i == pl.num_programs(0) - 1)
    def _():
        taps = res.shape[1] // cols
        acc = p_ref[0:spectra, :, 0:cols]
        for m in range(1, taps):
            acc = acc + p_ref[m : m + spectra, :, m * cols : (m + 1) * cols]
        o_ref[...] = acc


def frame_products(voltages, weights, fft_length, group, spectra):
    rows, samples = voltages.shape
    frames = samples // fft_length
    steps = -(-frames // group)
    width, _ = weights.shape
    cols = width // (frames - spectra + 1)
    return pl.pallas_call(
        _frame_kernel,
        grid=(steps,),
        in_specs=[
            pl.BlockSpec((rows, group * fft_length), lambda f: (0, f)),
            pl.BlockSpec((width, fft_length), lambda f: (0, 0)),
        ],
        out_specs=pl.BlockSpec((spectra, rows, cols), lambda f: (0, 0, 0)),
        out_shape=jax.ShapeDtypeStruct((spectra, rows, cols), jnp.float32),
        scratch_shapes=[pltpu.VMEM((steps * group, rows, width), jnp.float32)],
        compiler_params=pltpu.CompilerParams(vmem_limit_bytes=56 * 1024 * 1024),
    )(voltages, weights)


def channelize(voltages, filter_taps, channel_index):
    tap_count, fft_length = filter_taps.shape
    frame_count = voltages.shape[1] // fft_length
    spectra = frame_count - tap_count + 1
    twiddle = phase_table_t(channel_index, fft_length).astype(jnp.float32)
    cols = twiddle.shape[0]
    weights = (filter_taps[:, None, :] * twiddle[None, :, :]).astype(jnp.bfloat16)
    weights = weights.reshape(tap_count * cols, fft_length)
    return frame_products(voltages, weights, fft_length, 4, spectra)


def slot_index(antenna_slot_order):
    count = antenna_slot_order.shape[0]
    ids = jnp.arange(count, dtype=jnp.int32)
    return jnp.sum(
        jnp.where(antenna_slot_order[None, :] == ids[:, None], ids[None, :], 0), axis=1
    )


def _perm_kernel(inv_ref, mine_hbm, other_hbm, o_ref, e_ref, sem):
    pieces, block, _ = mine_hbm.shape
    line = (pieces + 1) // 2
    me = lax.axis_index("blk")
    pos, core = me // 2, me % 2

    def place(j):
        if j == 0:
            return pos
        if j < line:
            return pos - j
        return pos + (j - line + 1)

    copies = []
    for j in range(pieces):
        z = place(j)
        ok = jnp.logical_and(z >= 0, z < line)
        zc = jnp.clip(z, 0, line - 1)
        for k, (src, c) in enumerate(((mine_hbm, core), (other_hbm, 1 - core))):
            copy = pltpu.make_async_copy(
                src.at[j], e_ref.at[pl.ds((zc * 2 + c) * block, block)], sem.at[j, k]
            )
            copies.append((ok, copy))

            @pl.when(ok)
            def _():
                copy.start()

    for ok, copy in copies:

        @pl.when(ok)
        def _():
            copy.wait()

    def body(a, carry):
        src = inv_ref[a] * 2
        o_ref[pl.ds(2 * a, 2), :] = e_ref[pl.ds(src, 2), :]
        return carry

    lax.fori_loop(0, inv_ref.shape[0], body, 0, unroll=8)


def permute_pairs(mine, other, inverse):
    pieces, block, width = mine.shape
    rows = (pieces + 1) * block
    return pl.pallas_call(
        _perm_kernel,
        grid_spec=pltpu.PrefetchScalarGridSpec(
            num_scalar_prefetch=1,
            grid=(1,),
            in_specs=[pl.BlockSpec(memory_space=pl.ANY), pl.BlockSpec(memory_space=pl.ANY)],
            out_specs=pl.BlockSpec((rows, width), lambda i, inv: (0, 0)),
            scratch_shapes=[
                pltpu.VMEM((rows, width), mine.dtype),
                pltpu.SemaphoreType.DMA((pieces, 2)),
            ],
        ),
        out_shape=jax.ShapeDtypeStruct((rows, width), mine.dtype),
    )(inverse, mine, other)


def split2(x):
    hi = x.astype(jnp.bfloat16)
    lo = (x - hi.astype(jnp.float32)).astype(jnp.bfloat16)
    return hi, lo


def _corr_kernel(l_ref, o_ref, out_ref):
    res = jnp.dot(l_ref[0], o_ref[0], preferred_element_type=jnp.float32)
    out_ref[0] = res.astype(out_ref.dtype).reshape(out_ref.shape[1:])


def correlate(lhs, rhs, block_rows):
    chans, slots, pairs, width = lhs.shape
    cols = rhs.shape[2]
    lhs = lhs.reshape(chans, slots * pairs, width)
    return pl.pallas_call(
        _corr_kernel,
        grid=(chans, slots // block_rows),
        in_specs=[
            pl.BlockSpec((1, block_rows * pairs, width), lambda c, s: (c, s, 0)),
            pl.BlockSpec((1, width, cols), lambda c, s: (c, 0, 0)),
        ],
        out_specs=pl.BlockSpec((1, block_rows, pairs, cols), lambda c, s: (c, s, 0, 0)),
        out_shape=jax.ShapeDtypeStruct((chans, slots, pairs, cols), jnp.bfloat16),
        compiler_params=pltpu.CompilerParams(vmem_limit_bytes=48 * 1024 * 1024),
    )(lhs, rhs)


def exchange_channels(x, grp, local_ch):
    me = lax.axis_index("grp")
    got = []
    for d in range(grp):
        part = lax.dynamic_slice_in_dim(x, ((me + d) % grp) * local_ch, local_ch, axis=1)
        if d:
            part = lax.ppermute(part, "grp", [(j, (j + d) % grp) for j in range(grp)])
        got.append(part)
    stacked = jnp.stack(got, axis=0)
    order = (me - jnp.arange(grp, dtype=jnp.int32)) % grp
    stacked = jnp.take(stacked, order, axis=0)
    return stacked.reshape((grp * x.shape[0],) + stacked.shape[2:])


def gather_blocks(x):
    count = lax.psum(1, "blk")
    line = count // 2
    me = lax.axis_index("blk")
    pos, core = me // 2, me % 2
    right = [(z * 2 + c, (z + 1) * 2 + c) for z in range(line - 1) for c in range(2)]
    left = [(z * 2 + c, (z - 1) * 2 + c) for z in range(1, line) for c in range(2)]
    got_r, got_l = [], []
    r = x
    l = x
    for _ in range(1, line):
        r = lax.ppermute(r, "blk", right)
        l = lax.ppermute(l, "blk", left)
        got_r.append(r)
        got_l.append(l)
    cands = jnp.stack([x] + got_r + got_l, axis=0)
    other = lax.ppermute(cands, "blk", [(b, b ^ 1) for b in range(count)])
    return cands, other


def per_device(voltages, filter_taps, channel_index, antenna_slot_order):
    spec = channelize(voltages, filter_taps, channel_index)
    spectra, rows, cols = spec.shape
    chans = cols // 2
    grp = lax.psum(1, "grp")
    local_ch = chans // grp
    x = spec.reshape(spectra, rows, 2, chans).transpose(1, 3, 2, 0)
    x = exchange_channels(x, grp, local_ch)
    slots_local = x.shape[0]
    x = x.reshape(slots_local, local_ch * 2 * spectra)
    cands, other = gather_blocks(x)
    inverse = slot_index(antenna_slot_order)
    ordered = permute_pairs(cands, other, inverse)
    ordered = ordered.reshape(-1, local_ch, 2 * spectra).transpose(1, 0, 2)
    scale = jnp.float32(1.0 / spectra)
    xl = x.reshape(slots_local, local_ch, 2, spectra).transpose(1, 0, 2, 3) * scale
    re = xl[:, :, 0, :]
    im = xl[:, :, 1, :]
    row0 = jnp.concatenate([re, im], axis=-1)
    row1 = jnp.concatenate([im, -re], axis=-1)
    lhs = jnp.stack([row0, row1], axis=2)
    la, lb = split2(lhs)
    o1, o2 = split2(ordered)
    lcat = jnp.concatenate([la, la, lb], axis=-1)
    rhs = jnp.concatenate([o1, o2, o1], axis=-1).transpose(0, 2, 1)
    result = correlate(lcat, rhs, min(256, slots_local))
    return result


def solution(mesh):
    in_specs = (P(("blk", "grp"), None), P(), P(), P())
    out_specs = P("grp", "blk", None, None)
    return jax.shard_map(
        per_device, mesh=mesh, in_specs=in_specs, out_specs=out_specs, check_vma=False
    )
```

```python
import math

import jax
import jax.numpy as jnp
from jax import lax
from jax.experimental import pallas as pl
from jax.experimental.pallas import tpu as pltpu
from jax.sharding import PartitionSpec as P


def phase_table(channel_index, fft_length):
    samples_idx = jnp.arange(fft_length, dtype=jnp.int32)
    phase = samples_idx[:, None] * channel_index[None, :] % fft_length
    angle = phase.astype(jnp.float32) * jnp.float32(2.0 * math.pi / fft_length)
    return jnp.concatenate([jnp.cos(angle), -jnp.sin(angle)], axis=1).astype(jnp.bfloat16)


def phase_table_t(channel_index, fft_length):
    samples_idx = jnp.arange(fft_length, dtype=jnp.int32)
    phase = channel_index[:, None] * samples_idx[None, :] % fft_length
    angle = phase.astype(jnp.float32) * jnp.float32(2.0 * math.pi / fft_length)
    return jnp.concatenate([jnp.cos(angle), -jnp.sin(angle)], axis=0).astype(jnp.bfloat16)


def _frame_kernel(v_ref, w_ref, o_ref, p_ref):
    i = pl.program_id(0)
    n = w_ref.shape[1]
    spectra, rows, cols = o_ref.shape
    group = p_ref.shape[0] // pl.num_programs(0)
    lhs = jnp.concatenate([v_ref[:, g * n : (g + 1) * n] for g in range(group)], axis=0)
    res = lax.dot_general(
        lhs, w_ref[...], (((1,), (1,)), ((), ())), preferred_element_type=jnp.float32
    )
    p_ref[pl.ds(i * group, group)] = res.reshape(group, rows, res.shape[1])

    @pl.when(i == pl.num_programs(0) - 1)
    def _():
        taps = res.shape[1] // cols
        acc = p_ref[0:spectra, :, 0:cols]
        for m in range(1, taps):
            acc = acc + p_ref[m : m + spectra, :, m * cols : (m + 1) * cols]
        o_ref[...] = acc


def frame_products(voltages, weights, fft_length, group, spectra):
    rows, samples = voltages.shape
    frames = samples // fft_length
    steps = -(-frames // group)
    width, _ = weights.shape
    cols = width // (frames - spectra + 1)
    return pl.pallas_call(
        _frame_kernel,
        grid=(steps,),
        in_specs=[
            pl.BlockSpec((rows, group * fft_length), lambda f: (0, f)),
            pl.BlockSpec((width, fft_length), lambda f: (0, 0)),
        ],
        out_specs=pl.BlockSpec((spectra, rows, cols), lambda f: (0, 0, 0)),
        out_shape=jax.ShapeDtypeStruct((spectra, rows, cols), jnp.float32),
        scratch_shapes=[pltpu.VMEM((steps * group, rows, width), jnp.float32)],
        compiler_params=pltpu.CompilerParams(vmem_limit_bytes=56 * 1024 * 1024),
    )(voltages, weights)


def channelize(voltages, filter_taps, channel_index):
    tap_count, fft_length = filter_taps.shape
    frame_count = voltages.shape[1] // fft_length
    spectra = frame_count - tap_count + 1
    twiddle = phase_table_t(channel_index, fft_length).astype(jnp.float32)
    cols = twiddle.shape[0]
    weights = (filter_taps[:, None, :] * twiddle[None, :, :]).astype(jnp.bfloat16)
    weights = weights.reshape(tap_count * cols, fft_length)
    return frame_products(voltages, weights, fft_length, 4, spectra)


def slot_index(antenna_slot_order):
    count = antenna_slot_order.shape[0]
    ids = jnp.arange(count, dtype=jnp.int32)
    return jnp.sum(
        jnp.where(antenna_slot_order[None, :] == ids[:, None], ids[None, :], 0), axis=1
    )


def _perm_kernel(inv_ref, mine_hbm, other_hbm, o_ref, e_ref, sem):
    pieces, block, _ = mine_hbm.shape
    line = (pieces + 1) // 2
    me = lax.axis_index("blk")
    pos, core = me // 2, me % 2

    def place(j):
        if j == 0:
            return pos
        if j < line:
            return pos - j
        return pos + (j - line + 1)

    copies = []
    for j in range(pieces):
        z = place(j)
        ok = jnp.logical_and(z >= 0, z < line)
        zc = jnp.clip(z, 0, line - 1)
        for k, (src, c) in enumerate(((mine_hbm, core), (other_hbm, 1 - core))):
            copy = pltpu.make_async_copy(
                src.at[j], e_ref.at[pl.ds((zc * 2 + c) * block, block)], sem.at[j, k]
            )
            copies.append((ok, copy))

            @pl.when(ok)
            def _():
                copy.start()

    for ok, copy in copies:

        @pl.when(ok)
        def _():
            copy.wait()

    def body(a, carry):
        src = inv_ref[a] * 2
        o_ref[pl.ds(2 * a, 2), :] = e_ref[pl.ds(src, 2), :]
        return carry

    lax.fori_loop(0, inv_ref.shape[0], body, 0, unroll=8)


def permute_pairs(mine, other, inverse):
    pieces, block, width = mine.shape
    rows = (pieces + 1) * block
    return pl.pallas_call(
        _perm_kernel,
        grid_spec=pltpu.PrefetchScalarGridSpec(
            num_scalar_prefetch=1,
            grid=(1,),
            in_specs=[pl.BlockSpec(memory_space=pl.ANY), pl.BlockSpec(memory_space=pl.ANY)],
            out_specs=pl.BlockSpec((rows, width), lambda i, inv: (0, 0)),
            scratch_shapes=[
                pltpu.VMEM((rows, width), mine.dtype),
                pltpu.SemaphoreType.DMA((pieces, 2)),
            ],
        ),
        out_shape=jax.ShapeDtypeStruct((rows, width), mine.dtype),
    )(inverse, mine, other)


def split2(x):
    hi = x.astype(jnp.bfloat16)
    lo = (x - hi.astype(jnp.float32)).astype(jnp.bfloat16)
    return hi, lo


def _corr_kernel(l_ref, o_ref, out_ref):
    res = jnp.dot(l_ref[0], o_ref[0], preferred_element_type=jnp.float32)
    out_ref[0] = res.astype(out_ref.dtype).reshape(out_ref.shape[1:])


def correlate(lhs, rhs, block_rows):
    chans, slots, pairs, width = lhs.shape
    cols = rhs.shape[2]
    lhs = lhs.reshape(chans, slots * pairs, width)
    return pl.pallas_call(
        _corr_kernel,
        grid=(chans, slots // block_rows),
        in_specs=[
            pl.BlockSpec((1, block_rows * pairs, width), lambda c, s: (c, s, 0)),
            pl.BlockSpec((1, width, cols), lambda c, s: (c, 0, 0)),
        ],
        out_specs=pl.BlockSpec((1, block_rows, pairs, cols), lambda c, s: (c, s, 0, 0)),
        out_shape=jax.ShapeDtypeStruct((chans, slots, pairs, cols), jnp.bfloat16),
        compiler_params=pltpu.CompilerParams(vmem_limit_bytes=48 * 1024 * 1024),
    )(lhs, rhs)


def exchange_channels(x, grp, local_ch):
    me = lax.axis_index("grp")
    got = []
    for d in range(grp):
        part = lax.dynamic_slice_in_dim(x, ((me + d) % grp) * local_ch, local_ch, axis=1)
        if d:
            part = lax.ppermute(part, "grp", [(j, (j + d) % grp) for j in range(grp)])
        got.append(part)
    stacked = jnp.stack(got, axis=0)
    order = (me - jnp.arange(grp, dtype=jnp.int32)) % grp
    stacked = jnp.take(stacked, order, axis=0)
    return stacked.reshape((grp * x.shape[0],) + stacked.shape[2:])


def gather_blocks(x):
    count = lax.psum(1, "blk")
    line = count // 2
    me = lax.axis_index("blk")
    pos, core = me // 2, me % 2
    got_r, got_l = [], []
    for s in range(1, line):
        right = [(z * 2 + c, (z + s) * 2 + c) for z in range(line - s) for c in range(2)]
        left = [(z * 2 + c, (z - s) * 2 + c) for z in range(s, line) for c in range(2)]
        got_r.append(lax.ppermute(x, "blk", right))
        got_l.append(lax.ppermute(x, "blk", left))
    cands = jnp.stack([x] + got_r + got_l, axis=0)
    other = lax.ppermute(cands, "blk", [(b, b ^ 1) for b in range(count)])
    return cands, other


def per_device(voltages, filter_taps, channel_index, antenna_slot_order):
    spec = channelize(voltages, filter_taps, channel_index)
    spectra, rows, cols = spec.shape
    chans = cols // 2
    grp = lax.psum(1, "grp")
    local_ch = chans // grp
    x = spec.reshape(spectra, rows, 2, chans).transpose(1, 3, 2, 0)
    x = exchange_channels(x, grp, local_ch)
    slots_local = x.shape[0]
    x = x.reshape(slots_local, local_ch * 2 * spectra)
    cands, other = gather_blocks(x)
    inverse = slot_index(antenna_slot_order)
    ordered = permute_pairs(cands, other, inverse)
    ordered = ordered.reshape(-1, local_ch, 2 * spectra).transpose(1, 0, 2)
    scale = jnp.float32(1.0 / spectra)
    xl = x.reshape(slots_local, local_ch, 2, spectra).transpose(1, 0, 2, 3) * scale
    re = xl[:, :, 0, :]
    im = xl[:, :, 1, :]
    row0 = jnp.concatenate([re, im], axis=-1)
    row1 = jnp.concatenate([im, -re], axis=-1)
    lhs = jnp.stack([row0, row1], axis=2)
    la, lb = split2(lhs)
    o1, o2 = split2(ordered)
    lcat = jnp.concatenate([la, la, lb], axis=-1)
    rhs = jnp.concatenate([o1, o2, o1], axis=-1).transpose(0, 2, 1)
    result = correlate(lcat, rhs, min(256, slots_local))
    return result


def solution(mesh):
    in_specs = (P(("blk", "grp"), None), P(), P(), P())
    out_specs = P("grp", "blk", None, None)
    return jax.shard_map(
        per_device, mesh=mesh, in_specs=in_specs, out_specs=out_specs, check_vma=False
    )
```

```python
import math

import jax
import jax.numpy as jnp
from jax import lax
from jax.experimental import pallas as pl
from jax.experimental.pallas import tpu as pltpu
from jax.sharding import PartitionSpec as P


def phase_table(channel_index, fft_length):
    samples_idx = jnp.arange(fft_length, dtype=jnp.int32)
    phase = samples_idx[:, None] * channel_index[None, :] % fft_length
    angle = phase.astype(jnp.float32) * jnp.float32(2.0 * math.pi / fft_length)
    return jnp.concatenate([jnp.cos(angle), -jnp.sin(angle)], axis=1).astype(jnp.bfloat16)


def phase_table_t(channel_index, fft_length):
    samples_idx = jnp.arange(fft_length, dtype=jnp.int32)
    phase = channel_index[:, None] * samples_idx[None, :] % fft_length
    angle = phase.astype(jnp.float32) * jnp.float32(2.0 * math.pi / fft_length)
    return jnp.concatenate([jnp.cos(angle), -jnp.sin(angle)], axis=0).astype(jnp.bfloat16)


def _frame_kernel(v_ref, w_ref, o_ref, p_ref):
    i = pl.program_id(0)
    n = w_ref.shape[1]
    spectra, rows, cols = o_ref.shape
    group = p_ref.shape[0] // pl.num_programs(0)
    lhs = jnp.concatenate([v_ref[:, g * n : (g + 1) * n] for g in range(group)], axis=0)
    res = lax.dot_general(
        lhs, w_ref[...], (((1,), (1,)), ((), ())), preferred_element_type=jnp.float32
    )
    p_ref[pl.ds(i * group, group)] = res.reshape(group, rows, res.shape[1])

    @pl.when(i == pl.num_programs(0) - 1)
    def _():
        taps = res.shape[1] // cols
        acc = p_ref[0:spectra, :, 0:cols]
        for m in range(1, taps):
            acc = acc + p_ref[m : m + spectra, :, m * cols : (m + 1) * cols]
        o_ref[...] = acc


def frame_products(voltages, weights, fft_length, group, spectra):
    rows, samples = voltages.shape
    frames = samples // fft_length
    steps = -(-frames // group)
    width, _ = weights.shape
    cols = width // (frames - spectra + 1)
    return pl.pallas_call(
        _frame_kernel,
        grid=(steps,),
        in_specs=[
            pl.BlockSpec((rows, group * fft_length), lambda f: (0, f)),
            pl.BlockSpec((width, fft_length), lambda f: (0, 0)),
        ],
        out_specs=pl.BlockSpec((spectra, rows, cols), lambda f: (0, 0, 0)),
        out_shape=jax.ShapeDtypeStruct((spectra, rows, cols), jnp.float32),
        scratch_shapes=[pltpu.VMEM((steps * group, rows, width), jnp.float32)],
        compiler_params=pltpu.CompilerParams(vmem_limit_bytes=56 * 1024 * 1024),
    )(voltages, weights)


def channelize(voltages, filter_taps, channel_index):
    tap_count, fft_length = filter_taps.shape
    frame_count = voltages.shape[1] // fft_length
    spectra = frame_count - tap_count + 1
    twiddle = phase_table_t(channel_index, fft_length).astype(jnp.float32)
    cols = twiddle.shape[0]
    weights = (filter_taps[:, None, :] * twiddle[None, :, :]).astype(jnp.bfloat16)
    weights = weights.reshape(tap_count * cols, fft_length)
    return frame_products(voltages, weights, fft_length, 4, spectra)


def slot_index(antenna_slot_order):
    count = antenna_slot_order.shape[0]
    ids = jnp.arange(count, dtype=jnp.int32)
    return jnp.sum(
        jnp.where(antenna_slot_order[None, :] == ids[:, None], ids[None, :], 0), axis=1
    )


def _perm_kernel(inv_ref, mine_hbm, other_hbm, o_ref, e_ref, sem):
    pieces, block, _ = mine_hbm.shape
    line = (pieces + 1) // 2
    me = lax.axis_index("blk")
    pos, core = me // 2, me % 2

    def place(j):
        if j == 0:
            return pos
        if j < line:
            return pos - j
        return pos + (j - line + 1)

    copies = []
    for j in range(pieces):
        z = place(j)
        ok = jnp.logical_and(z >= 0, z < line)
        zc = jnp.clip(z, 0, line - 1)
        for k, (src, c) in enumerate(((mine_hbm, core), (other_hbm, 1 - core))):
            copy = pltpu.make_async_copy(
                src.at[j], e_ref.at[pl.ds((zc * 2 + c) * block, block)], sem.at[j, k]
            )
            copies.append((ok, copy))

            @pl.when(ok)
            def _():
                copy.start()

    for ok, copy in copies:

        @pl.when(ok)
        def _():
            copy.wait()

    def body(a, carry):
        src = inv_ref[a] * 2
        o_ref[pl.ds(2 * a, 2), :] = e_ref[pl.ds(src, 2), :]
        return carry

    lax.fori_loop(0, inv_ref.shape[0], body, 0, unroll=16)


def permute_pairs(mine, other, inverse):
    pieces, block, width = mine.shape
    rows = (pieces + 1) * block
    return pl.pallas_call(
        _perm_kernel,
        grid_spec=pltpu.PrefetchScalarGridSpec(
            num_scalar_prefetch=1,
            grid=(1,),
            in_specs=[pl.BlockSpec(memory_space=pl.ANY), pl.BlockSpec(memory_space=pl.ANY)],
            out_specs=pl.BlockSpec((rows, width), lambda i, inv: (0, 0)),
            scratch_shapes=[
                pltpu.VMEM((rows, width), mine.dtype),
                pltpu.SemaphoreType.DMA((pieces, 2)),
            ],
        ),
        out_shape=jax.ShapeDtypeStruct((rows, width), mine.dtype),
    )(inverse, mine, other)


def split2(x):
    hi = x.astype(jnp.bfloat16)
    lo = (x - hi.astype(jnp.float32)).astype(jnp.bfloat16)
    return hi, lo


def _corr_kernel(l_ref, o_ref, out_ref):
    res = jnp.dot(l_ref[0], o_ref[0], preferred_element_type=jnp.float32)
    out_ref[0] = res.astype(out_ref.dtype).reshape(out_ref.shape[1:])


def correlate(lhs, rhs, block_rows):
    chans, slots, pairs, width = lhs.shape
    cols = rhs.shape[2]
    lhs = lhs.reshape(chans, slots * pairs, width)
    return pl.pallas_call(
        _corr_kernel,
        grid=(chans, slots // block_rows),
        in_specs=[
            pl.BlockSpec((1, block_rows * pairs, width), lambda c, s: (c, s, 0)),
            pl.BlockSpec((1, width, cols), lambda c, s: (c, 0, 0)),
        ],
        out_specs=pl.BlockSpec((1, block_rows, pairs, cols), lambda c, s: (c, s, 0, 0)),
        out_shape=jax.ShapeDtypeStruct((chans, slots, pairs, cols), jnp.bfloat16),
        compiler_params=pltpu.CompilerParams(vmem_limit_bytes=48 * 1024 * 1024),
    )(lhs, rhs)


def exchange_channels(x, grp, local_ch):
    me = lax.axis_index("grp")
    got = []
    for d in range(grp):
        part = lax.dynamic_slice_in_dim(x, ((me + d) % grp) * local_ch, local_ch, axis=1)
        if d:
            part = lax.ppermute(part, "grp", [(j, (j + d) % grp) for j in range(grp)])
        got.append(part)
    stacked = jnp.stack(got, axis=0)
    order = (me - jnp.arange(grp, dtype=jnp.int32)) % grp
    stacked = jnp.take(stacked, order, axis=0)
    return stacked.reshape((grp * x.shape[0],) + stacked.shape[2:])


def gather_blocks(x):
    count = lax.psum(1, "blk")
    line = count // 2
    me = lax.axis_index("blk")
    pos, core = me // 2, me % 2
    right = [(z * 2 + c, (z + 1) * 2 + c) for z in range(line - 1) for c in range(2)]
    left = [(z * 2 + c, (z - 1) * 2 + c) for z in range(1, line) for c in range(2)]
    got_r, got_l = [], []
    r = x
    l = x
    for _ in range(1, line):
        r = lax.ppermute(r, "blk", right)
        l = lax.ppermute(l, "blk", left)
        got_r.append(r)
        got_l.append(l)
    cands = jnp.stack([x] + got_r + got_l, axis=0)
    other = lax.ppermute(cands, "blk", [(b, b ^ 1) for b in range(count)])
    return cands, other


def per_device(voltages, filter_taps, channel_index, antenna_slot_order):
    spec = channelize(voltages, filter_taps, channel_index)
    spectra, rows, cols = spec.shape
    chans = cols // 2
    grp = lax.psum(1, "grp")
    local_ch = chans // grp
    x = spec.reshape(spectra, rows, 2, chans).transpose(1, 3, 2, 0)
    x = exchange_channels(x, grp, local_ch)
    slots_local = x.shape[0]
    x = x.reshape(slots_local, local_ch * 2 * spectra)
    cands, other = gather_blocks(x)
    inverse = slot_index(antenna_slot_order)
    ordered = permute_pairs(cands, other, inverse)
    ordered = ordered.reshape(-1, local_ch, 2 * spectra).transpose(1, 0, 2)
    scale = jnp.float32(1.0 / spectra)
    xl = x.reshape(slots_local, local_ch, 2, spectra).transpose(1, 0, 2, 3) * scale
    re = xl[:, :, 0, :]
    im = xl[:, :, 1, :]
    row0 = jnp.concatenate([re, im], axis=-1)
    row1 = jnp.concatenate([im, -re], axis=-1)
    lhs = jnp.stack([row0, row1], axis=2)
    la, lb = split2(lhs)
    o1, o2 = split2(ordered)
    lcat = jnp.concatenate([la, la, lb], axis=-1)
    rhs = jnp.concatenate([o1, o2, o1], axis=-1).transpose(0, 2, 1)
    result = correlate(lcat, rhs, min(512, slots_local))
    return result


def solution(mesh):
    in_specs = (P(("blk", "grp"), None), P(), P(), P())
    out_specs = P("grp", "blk", None, None)
    return jax.shard_map(
        per_device, mesh=mesh, in_specs=in_specs, out_specs=out_specs, check_vma=False
    )
```

```python
import math

import jax
import jax.numpy as jnp
from jax import lax
from jax.experimental import pallas as pl
from jax.experimental.pallas import tpu as pltpu
from jax.sharding import PartitionSpec as P


def phase_table(channel_index, fft_length):
    samples_idx = jnp.arange(fft_length, dtype=jnp.int32)
    phase = samples_idx[:, None] * channel_index[None, :] % fft_length
    angle = phase.astype(jnp.float32) * jnp.float32(2.0 * math.pi / fft_length)
    return jnp.concatenate([jnp.cos(angle), -jnp.sin(angle)], axis=1).astype(jnp.bfloat16)


def phase_table_t(channel_index, fft_length):
    samples_idx = jnp.arange(fft_length, dtype=jnp.int32)
    phase = channel_index[:, None] * samples_idx[None, :] % fft_length
    angle = phase.astype(jnp.float32) * jnp.float32(2.0 * math.pi / fft_length)
    return jnp.concatenate([jnp.cos(angle), -jnp.sin(angle)], axis=0).astype(jnp.bfloat16)


def _frame_kernel(v_ref, w_ref, o_ref, p_ref):
    i = pl.program_id(0)
    n = w_ref.shape[1]
    spectra, rows, cols = o_ref.shape
    group = p_ref.shape[0] // pl.num_programs(0)
    lhs = jnp.concatenate([v_ref[:, g * n : (g + 1) * n] for g in range(group)], axis=0)
    res = lax.dot_general(
        lhs, w_ref[...], (((1,), (1,)), ((), ())), preferred_element_type=jnp.float32
    )
    p_ref[pl.ds(i * group, group)] = res.reshape(group, rows, res.shape[1])

    @pl.when(i == pl.num_programs(0) - 1)
    def _():
        taps = res.shape[1] // cols
        acc = p_ref[0:spectra, :, 0:cols]
        for m in range(1, taps):
            acc = acc + p_ref[m : m + spectra, :, m * cols : (m + 1) * cols]
        o_ref[...] = acc


def frame_products(voltages, weights, fft_length, group, spectra):
    rows, samples = voltages.shape
    frames = samples // fft_length
    steps = -(-frames // group)
    width, _ = weights.shape
    cols = width // (frames - spectra + 1)
    return pl.pallas_call(
        _frame_kernel,
        grid=(steps,),
        in_specs=[
            pl.BlockSpec((rows, group * fft_length), lambda f: (0, f)),
            pl.BlockSpec((width, fft_length), lambda f: (0, 0)),
        ],
        out_specs=pl.BlockSpec((spectra, rows, cols), lambda f: (0, 0, 0)),
        out_shape=jax.ShapeDtypeStruct((spectra, rows, cols), jnp.float32),
        scratch_shapes=[pltpu.VMEM((steps * group, rows, width), jnp.float32)],
        compiler_params=pltpu.CompilerParams(vmem_limit_bytes=56 * 1024 * 1024),
    )(voltages, weights)


def channelize(voltages, filter_taps, channel_index):
    tap_count, fft_length = filter_taps.shape
    frame_count = voltages.shape[1] // fft_length
    spectra = frame_count - tap_count + 1
    twiddle = phase_table_t(channel_index, fft_length).astype(jnp.float32)
    cols = twiddle.shape[0]
    weights = (filter_taps[:, None, :] * twiddle[None, :, :]).astype(jnp.bfloat16)
    weights = weights.reshape(tap_count * cols, fft_length)
    return frame_products(voltages, weights, fft_length, 6, spectra)


def slot_index(antenna_slot_order):
    count = antenna_slot_order.shape[0]
    ids = jnp.arange(count, dtype=jnp.int32)
    return jnp.sum(
        jnp.where(antenna_slot_order[None, :] == ids[:, None], ids[None, :], 0), axis=1
    )


def _perm_kernel(inv_ref, mine_hbm, other_hbm, o_ref, e_ref, sem):
    pieces, block, _ = mine_hbm.shape
    line = (pieces + 1) // 2
    me = lax.axis_index("blk")
    pos, core = me // 2, me % 2

    def place(j):
        if j == 0:
            return pos
        if j < line:
            return pos - j
        return pos + (j - line + 1)

    copies = []
    for j in range(pieces):
        z = place(j)
        ok = jnp.logical_and(z >= 0, z < line)
        zc = jnp.clip(z, 0, line - 1)
        for k, (src, c) in enumerate(((mine_hbm, core), (other_hbm, 1 - core))):
            copy = pltpu.make_async_copy(
                src.at[j], e_ref.at[pl.ds((zc * 2 + c) * block, block)], sem.at[j, k]
            )
            copies.append((ok, copy))

            @pl.when(ok)
            def _():
                copy.start()

    for ok, copy in copies:

        @pl.when(ok)
        def _():
            copy.wait()

    def body(a, carry):
        src = inv_ref[a] * 2
        o_ref[pl.ds(2 * a, 2), :] = e_ref[pl.ds(src, 2), :]
        return carry

    lax.fori_loop(0, inv_ref.shape[0], body, 0, unroll=16)


def permute_pairs(mine, other, inverse):
    pieces, block, width = mine.shape
    rows = (pieces + 1) * block
    return pl.pallas_call(
        _perm_kernel,
        grid_spec=pltpu.PrefetchScalarGridSpec(
            num_scalar_prefetch=1,
            grid=(1,),
            in_specs=[pl.BlockSpec(memory_space=pl.ANY), pl.BlockSpec(memory_space=pl.ANY)],
            out_specs=pl.BlockSpec((rows, width), lambda i, inv: (0, 0)),
            scratch_shapes=[
                pltpu.VMEM((rows, width), mine.dtype),
                pltpu.SemaphoreType.DMA((pieces, 2)),
            ],
        ),
        out_shape=jax.ShapeDtypeStruct((rows, width), mine.dtype),
    )(inverse, mine, other)


def split2(x):
    hi = x.astype(jnp.bfloat16)
    lo = (x - hi.astype(jnp.float32)).astype(jnp.bfloat16)
    return hi, lo


def _corr_kernel(l_ref, o_ref, out_ref):
    res = jnp.dot(l_ref[0], o_ref[0], preferred_element_type=jnp.float32)
    out_ref[0] = res.astype(out_ref.dtype).reshape(out_ref.shape[1:])


def correlate(lhs, rhs, block_rows):
    chans, slots, pairs, width = lhs.shape
    cols = rhs.shape[2]
    lhs = lhs.reshape(chans, slots * pairs, width)
    return pl.pallas_call(
        _corr_kernel,
        grid=(chans, slots // block_rows),
        in_specs=[
            pl.BlockSpec((1, block_rows * pairs, width), lambda c, s: (c, s, 0)),
            pl.BlockSpec((1, width, cols), lambda c, s: (c, 0, 0)),
        ],
        out_specs=pl.BlockSpec((1, block_rows, pairs, cols), lambda c, s: (c, s, 0, 0)),
        out_shape=jax.ShapeDtypeStruct((chans, slots, pairs, cols), jnp.bfloat16),
        compiler_params=pltpu.CompilerParams(vmem_limit_bytes=48 * 1024 * 1024),
    )(lhs, rhs)


def exchange_channels(x, grp, local_ch):
    me = lax.axis_index("grp")
    got = []
    for d in range(grp):
        part = lax.dynamic_slice_in_dim(x, ((me + d) % grp) * local_ch, local_ch, axis=1)
        if d:
            part = lax.ppermute(part, "grp", [(j, (j + d) % grp) for j in range(grp)])
        got.append(part)
    stacked = jnp.stack(got, axis=0)
    order = (me - jnp.arange(grp, dtype=jnp.int32)) % grp
    stacked = jnp.take(stacked, order, axis=0)
    return stacked.reshape((grp * x.shape[0],) + stacked.shape[2:])


def gather_blocks(x):
    count = lax.psum(1, "blk")
    line = count // 2
    me = lax.axis_index("blk")
    pos, core = me // 2, me % 2
    right = [(z * 2 + c, (z + 1) * 2 + c) for z in range(line - 1) for c in range(2)]
    left = [(z * 2 + c, (z - 1) * 2 + c) for z in range(1, line) for c in range(2)]
    got_r, got_l = [], []
    r = x
    l = x
    for _ in range(1, line):
        r = lax.ppermute(r, "blk", right)
        l = lax.ppermute(l, "blk", left)
        got_r.append(r)
        got_l.append(l)
    cands = jnp.stack([x] + got_r + got_l, axis=0)
    other = lax.ppermute(cands, "blk", [(b, b ^ 1) for b in range(count)])
    return cands, other


def per_device(voltages, filter_taps, channel_index, antenna_slot_order):
    spec = channelize(voltages, filter_taps, channel_index)
    spectra, rows, cols = spec.shape
    chans = cols // 2
    grp = lax.psum(1, "grp")
    local_ch = chans // grp
    x = spec.reshape(spectra, rows, 2, chans).transpose(1, 3, 2, 0)
    x = exchange_channels(x, grp, local_ch)
    slots_local = x.shape[0]
    x = x.reshape(slots_local, local_ch * 2 * spectra)
    cands, other = gather_blocks(x)
    inverse = slot_index(antenna_slot_order)
    ordered = permute_pairs(cands, other, inverse)
    ordered = ordered.reshape(-1, local_ch, 2 * spectra).transpose(1, 0, 2)
    scale = jnp.float32(1.0 / spectra)
    xl = x.reshape(slots_local, local_ch, 2, spectra).transpose(1, 0, 2, 3) * scale
    re = xl[:, :, 0, :]
    im = xl[:, :, 1, :]
    row0 = jnp.concatenate([re, im], axis=-1)
    row1 = jnp.concatenate([im, -re], axis=-1)
    lhs = jnp.stack([row0, row1], axis=2)
    la, lb = split2(lhs)
    o1, o2 = split2(ordered)
    lcat = jnp.concatenate([la, la, lb], axis=-1)
    rhs = jnp.concatenate([o1, o2, o1], axis=-1).transpose(0, 2, 1)
    result = correlate(lcat, rhs, min(512, slots_local))
    return result


def solution(mesh):
    in_specs = (P(("blk", "grp"), None), P(), P(), P())
    out_specs = P("grp", "blk", None, None)
    return jax.shard_map(
        per_device, mesh=mesh, in_specs=in_specs, out_specs=out_specs, check_vma=False
    )
```
